512 devices in a mesh: dp: 32 (over x, z_lo, core), ctx: 16 (over z_hi, y).
Axes of the slice: x: 4, y: 8, z: 8 (z_hi: 2, z_lo: 4; z = z_hi * 4 + z_lo), core: 2. Of those that a mesh axis runs over, the one named last changes fastest.
Arguments:
- queries: bfloat16 [32, 16, 128, 2048], P('dp', 'ctx'), may hold values from -2.5 to 2.5
- rotated_key_rows: bfloat16 [32, 16, 128, 512], P('dp', 'ctx'), may hold values from -2.5 to 2.5
- values: bfloat16 [32, 16, 128, 512], P('dp', 'ctx'), may hold values from -6 to 6
- cotangent: bfloat16 [32, 16, 128, 2048], P('dp', 'ctx'), may hold values from -6 to 6
- hidden: bfloat16 [32, 16, 128, 4096], P('dp', 'ctx'), may hold values from -6 to 6
- adapter_down_weight: bfloat16 [4096, 16], replicated, may hold values from -0.09375 to 0.09375
- adapter_up_weight: bfloat16 [16, 512], replicated, may hold values from -1.5 to 1.5
- segment_text_length: int32 [32, 16], P('dp', 'ctx'), may hold values from 19 to 78, as said below
Outputs:
- grad_queries: bfloat16 [32, 16, 128, 2048], P('dp', 'ctx')
- grad_keys: bfloat16 [32, 16, 128, 512], P('dp', 'ctx')
- grad_values: bfloat16 [32, 16, 128, 512], P('dp', 'ctx')
- grad_down: float32 [4096, 16], replicated
- grad_up: float32 [16, 512], replicated
The draws below stay inside these ranges and needn't reach their ends.
Inputs may be any that keep to these rules, and one draw needn't show every extreme that they name: `segment_text_length`: every log has a segment with exactly 78 text tokens and another with the fewest.
All inputs are finite; a program needn't handle non-finite values.
Results may differ from the reference program's by a relative error of at most 0.0019.
The reference program's roundings to bfloat16 on the way count: a program that leaves them out, or rounds other values in their place, can miss the bound.
Values may be sent and summed in bfloat16 or wider, within the bound.
No kernel may reach another device: no remote copies, remote signals or barrier semaphores. Data moves between devices by JAX's collectives and lax.ppermute only.
A program may use at most 64 MiB of HBM per device.

```python
import math
import jax
import jax.numpy as jnp
from jax import lax

MODEL_WIDTH = 4096
HQ = 16
KEY_VALUE_HEADS = 4
HEAD_SIZE = 128
SUMM = 50
ADAPTER_RANK = 16
TOK_DEV = 128
LOG_COUNT = 32
SEGMENT_COUNT = 16


def draw_segment_text_length(key, part):
    first, second = jax.random.split(key)
    lowest = (TOK_DEV - SUMM) // 4
    highest = TOK_DEV - SUMM
    base = jax.random.randint(first, (LOG_COUNT, SEGMENT_COUNT), lowest, highest + 1)
    chosen = jax.random.randint(second, (LOG_COUNT, 1), 0, SEGMENT_COUNT)
    columns = jnp.arange(SEGMENT_COUNT)[None, :]
    base = jnp.where(columns == chosen, highest, base)
    base = jnp.where(columns == (chosen + 1) % SEGMENT_COUNT, lowest, base)
    return base.astype(jnp.int32)


def steps_of(rng, extent, cuts, low, largest):
    gain, own = 1.0, jax.random.fold_in(rng, 6)
    for dim, shards_of in cuts:
        steps = jnp.exp(jax.random.uniform(jax.random.fold_in(own, dim), (shards_of,), jnp.float32, low / len(cuts), largest / len(cuts)))
        gain = gain * jnp.repeat(steps, extent[dim] // shards_of).reshape([-1 if axis == dim else 1 for axis in range(len(extent))])
    return gain


def bell_draw(stream_key, extent, spread, most, cuts=(), kind=jnp.bfloat16):
    entries = jax.random.normal(stream_key, extent, jnp.float32) * spread
    if len(cuts) > 0:
        entries = steps_of(stream_key, extent, cuts, -0.22, 0.18) * entries
    return jnp.clip(entries, min=-most, max=most).astype(kind)


def setup_inputs(seed: int = 0) -> dict:
    arg_keys = jax.random.split(jax.random.key(seed), 9)
    queries = bell_draw(arg_keys[0], (LOG_COUNT, SEGMENT_COUNT, TOK_DEV, HQ * HEAD_SIZE), 1.0, 2.5, ((0, 32), (1, 16)))
    rotated_key_rows = bell_draw(arg_keys[1], (LOG_COUNT, SEGMENT_COUNT, TOK_DEV, KEY_VALUE_HEADS * HEAD_SIZE), 1.0, 2.5, ((0, 32), (1, 16)))
    values = bell_draw(arg_keys[2], (LOG_COUNT, SEGMENT_COUNT, TOK_DEV, KEY_VALUE_HEADS * HEAD_SIZE), 1.0, 6.0, ((0, 32), (1, 16)))
    cotangent = bell_draw(arg_keys[3], (LOG_COUNT, SEGMENT_COUNT, TOK_DEV, HQ * HEAD_SIZE), 1.0, 6.0, ((0, 32), (1, 16)))
    hidden = bell_draw(arg_keys[4], (LOG_COUNT, SEGMENT_COUNT, TOK_DEV, MODEL_WIDTH), 1.0, 6.0, ((0, 32), (1, 16)))
    adapter_down_weight = bell_draw(arg_keys[5], (MODEL_WIDTH, ADAPTER_RANK), MODEL_WIDTH ** -0.5, 0.09375)
    adapter_up_weight = bell_draw(arg_keys[6], (ADAPTER_RANK, KEY_VALUE_HEADS * HEAD_SIZE), ADAPTER_RANK ** -0.5, 1.5)
    segment_text_length = draw_segment_text_length(jax.random.fold_in(arg_keys[8], 71), 0)
    return dict(queries=queries, rotated_key_rows=rotated_key_rows, values=values, cotangent=cotangent, hidden=hidden, adapter_down_weight=adapter_down_weight, adapter_up_weight=adapter_up_weight, segment_text_length=segment_text_length)


adapter_scale = 2.0

def low_copy(array):
    return lax.optimization_barrier(array.astype(jnp.bfloat16)).astype(jnp.float32)

def segment_grads(query_rows, key_local, value_local, cot_rows, memory_keys, memory_values, memory_owner, position, length):
    tokens = query_rows.shape[0]
    groups = HQ // KEY_VALUE_HEADS
    live = length + SUMM
    rows = jnp.arange(tokens).astype(jnp.int32)
    cot_rows = jnp.where((rows < live)[:, None], cot_rows, jnp.zeros_like(cot_rows))
    local_mask = (rows[None, :] <= rows[:, None]) & (rows[None, :] < live)
    memory_mask = jnp.broadcast_to((memory_owner < position)[None, :], (tokens, memory_owner.shape[0]))
    key_mask = jnp.concatenate([memory_mask, local_mask], axis=1)
    all_keys = jnp.concatenate([memory_keys, key_local], 0).reshape(-1, KEY_VALUE_HEADS, HEAD_SIZE).astype(jnp.float32)
    all_values = jnp.concatenate([memory_values, value_local], 0).reshape(-1, KEY_VALUE_HEADS, HEAD_SIZE).astype(jnp.float32)
    queries = query_rows.reshape(tokens, KEY_VALUE_HEADS, groups, HEAD_SIZE).astype(jnp.float32)
    cotangents = cot_rows.reshape(tokens, KEY_VALUE_HEADS, groups, HEAD_SIZE).astype(jnp.float32)
    softmax_scale = 1.0 / math.sqrt(HEAD_SIZE)
    scores = jnp.einsum('tkgd,mkd->kgtm', queries, all_keys) * softmax_scale
    unnorm = jnp.where(key_mask, jnp.exp(scores), 0.0)
    attend = unnorm / lax.optimization_barrier(jnp.sum(unnorm, -1, keepdims=True))
    attend_grad = jnp.einsum('tkgd,mkd->kgtm', cotangents, all_values)
    row_dot = lax.optimization_barrier(jnp.sum(attend * attend_grad, -1, keepdims=True))
    dscore = low_copy(attend * (attend_grad - row_dot))
    attend_low = low_copy(attend)
    query_grad = jnp.einsum('kgtm,mkd->tkgd', dscore, all_keys) * softmax_scale
    key_grad = jnp.einsum('kgtm,tkgd->mkd', dscore, queries) * softmax_scale
    value_grad = jnp.einsum('kgtm,tkgd->mkd', attend_low, cotangents)
    count = memory_keys.shape[0]
    key_grad = key_grad.reshape(-1, KEY_VALUE_HEADS * HEAD_SIZE)
    value_grad = value_grad.reshape(-1, KEY_VALUE_HEADS * HEAD_SIZE)
    return (query_grad.reshape(tokens, HQ * HEAD_SIZE).astype(jnp.bfloat16), key_grad[:count], key_grad[count:], value_grad[:count], value_grad[count:])

def reference(queries, rotated_key_rows, values, cotangent, hidden, adapter_down_weight, adapter_up_weight, segment_text_length):
    width = KEY_VALUE_HEADS * HEAD_SIZE

    def one_log(inputs):
        query_log, key_log, value_log, cot_log, hidden_log, length_log = inputs

        def take(rows, length):
            return lax.dynamic_slice_in_dim(rows, length, SUMM, 0)
        memory_keys = jax.vmap(take)(key_log, length_log).reshape(SEGMENT_COUNT * SUMM, width)
        memory_values = jax.vmap(take)(value_log, length_log).reshape(SEGMENT_COUNT * SUMM, width)
        memory_owner = (jnp.arange(SEGMENT_COUNT * SUMM) // SUMM).astype(jnp.int32)

        def one_segment(position):
            return segment_grads(query_log[position], key_log[position], value_log[position], cot_log[position], memory_keys, memory_values, memory_owner, position, length_log[position])
        query_grad, memory_key, local_key, memory_value, local_value = lax.map(one_segment, jnp.arange(SEGMENT_COUNT).astype(jnp.int32))
        back_key = lax.optimization_barrier(jnp.sum(memory_key, 0)).reshape(SEGMENT_COUNT, SUMM, width)
        back_value = lax.optimization_barrier(jnp.sum(memory_value, 0)).reshape(SEGMENT_COUNT, SUMM, width)

        def place(local, backward_step, length):
            return local + lax.dynamic_update_slice_in_dim(jnp.zeros_like(local), backward_step, length, 0)
        key_out = jax.vmap(place)(local_key, back_key, length_log).astype(jnp.bfloat16)
        value_result = jax.vmap(place)(local_value, back_value, length_log).astype(jnp.bfloat16)
        hidden_broad = hidden_log.astype(jnp.float32)
        low_rank_state = jnp.einsum('uwx,xe->uwe', hidden_broad, adapter_down_weight.astype(jnp.float32)).astype(jnp.bfloat16)
        backward_step = jnp.einsum('hig,og->hio', value_result.astype(jnp.float32), adapter_up_weight.astype(jnp.float32)).astype(jnp.bfloat16)
        down_part = jnp.einsum('std,str->dr', hidden_broad, backward_step.astype(jnp.float32))
        up_part = jnp.einsum('str,stc->rc', low_rank_state.astype(jnp.float32), value_result.astype(jnp.float32))
        return (query_grad, key_out, value_result, down_part, up_part)
    results = lax.map(one_log, (queries, rotated_key_rows, values, cotangent, hidden, segment_text_length))
    adapter_factor = adapter_scale / (LOG_COUNT * SEGMENT_COUNT)
    return (results[0], results[1], results[2], lax.optimization_barrier(jnp.sum(results[3], 0)) * adapter_factor, lax.optimization_barrier(jnp.sum(results[4], 0)) * adapter_factor)
```

```python
import math

import jax
import jax.numpy as jnp
from jax import lax
from jax.sharding import PartitionSpec as P

HEAD_SIZE = 128
SUMM = 50


adapter_scale = 2.0


def group_grads(query_group, key_group, value_group, cot_group, key_mask):
    softmax_scale = 1.0 / math.sqrt(HEAD_SIZE)
    scores = (
        jnp.einsum("tgd,md->gtm", query_group, key_group, preferred_element_type=jnp.float32)
        * softmax_scale
    )
    unnorm = jnp.exp(jnp.where(key_mask[None], scores, -jnp.inf))
    attend = unnorm / jnp.sum(unnorm, -1, keepdims=True)
    attend_grad = jnp.einsum(
        "tgd,md->gtm", cot_group, value_group, preferred_element_type=jnp.float32
    )
    row_dot = jnp.sum(attend * attend_grad, -1, keepdims=True)
    dscore = (attend * (attend_grad - row_dot)).astype(jnp.bfloat16)
    attend_low = attend.astype(jnp.bfloat16)
    query_grad = (
        jnp.einsum("gtm,md->tgd", dscore, key_group, preferred_element_type=jnp.float32)
        * softmax_scale
    )
    key_grad = (
        jnp.einsum("gtm,tgd->md", dscore, query_group, preferred_element_type=jnp.float32)
        * softmax_scale
    )
    value_grad = jnp.einsum(
        "gtm,tgd->md", attend_low, cot_group, preferred_element_type=jnp.float32
    )
    return (query_grad, key_grad, value_grad)


def adapter_terms(hidden_piece, low_rank_piece, value_piece, adapter_up_weight):
    contract = (((0,), (0,)), ((), ()))
    backward_step = lax.dot_general(
        value_piece, adapter_up_weight, (((1,), (1,)), ((), ())), preferred_element_type=jnp.float32
    ).astype(jnp.bfloat16)
    down_part_t = lax.dot_general(
        backward_step, hidden_piece, contract, preferred_element_type=jnp.float32
    )
    up_part = lax.dot_general(
        low_rank_piece, value_piece, contract, preferred_element_type=jnp.float32
    )
    return jnp.concatenate([down_part_t, up_part], 1)


def butterfly_sum(x, axis):
    n = lax.axis_size(axis)
    if n & (n - 1):
        return lax.psum(x, axis)
    k = 1
    while k < n:
        x = x + lax.ppermute(x, axis, [(i, i ^ k) for i in range(n)])
        k *= 2
    return x


def per_device(
    queries,
    rotated_key_rows,
    values,
    cotangent,
    hidden,
    adapter_down_weight,
    adapter_up_weight,
    segment_text_length,
):
    query_rows = queries[0, 0]
    key_local = rotated_key_rows[0, 0]
    value_local = values[0, 0]
    cot_rows = cotangent[0, 0]
    hidden_row_block = hidden[0, 0]
    length = segment_text_length[0, 0]
    position = lax.axis_index("ctx")
    segment_list = lax.axis_size("ctx")
    log_batch = lax.axis_size("dp")
    tokens = query_rows.shape[0]
    width = key_local.shape[1]
    kv_heads = width // HEAD_SIZE
    groups = query_rows.shape[1] // width
    live = length + SUMM
    rows = jnp.arange(tokens)
    cot_rows = jnp.where((rows < live)[:, None], cot_rows, jnp.zeros_like(cot_rows))
    own_keys = lax.dynamic_slice_in_dim(key_local, length, SUMM, 0)
    own_values = lax.dynamic_slice_in_dim(value_local, length, SUMM, 0)
    own_summary = jnp.concatenate([own_keys, own_values], 0)
    pieces = [own_summary] + [
        lax.ppermute(own_summary, "ctx", [(i, i + k) for i in range(segment_list - k)])
        for k in range(1, segment_list)
    ]
    slot_of_segment = (position - jnp.arange(segment_list)) % segment_list
    gathered = jnp.take(jnp.stack(pieces), slot_of_segment, axis=0).reshape(
        segment_list, 2, SUMM, width
    )
    memory_keys = gathered[:, 0].reshape(segment_list * SUMM, width)
    memory_values = gathered[:, 1].reshape(segment_list * SUMM, width)
    count = memory_keys.shape[0]
    memory_owner = jnp.arange(count) // SUMM
    local_mask = (rows[None, :] <= rows[:, None]) & (rows[None, :] < live)
    memory_mask = jnp.broadcast_to((memory_owner < position)[None, :], (tokens, count))
    key_mask = jnp.concatenate([memory_mask, local_mask], axis=1)
    all_keys = jnp.concatenate([memory_keys, key_local], 0)
    all_values = jnp.concatenate([memory_values, value_local], 0)
    query_parts, key_parts, value_parts = ([], [], [])
    for group in range(kv_heads):
        qcols = slice(group * groups * HEAD_SIZE, (group + 1) * groups * HEAD_SIZE)
        kcols = slice(group * HEAD_SIZE, (group + 1) * HEAD_SIZE)
        query_grad, key_grad, value_grad = group_grads(
            query_rows[:, qcols].reshape(tokens, groups, HEAD_SIZE),
            all_keys[:, kcols],
            all_values[:, kcols],
            cot_rows[:, qcols].reshape(tokens, groups, HEAD_SIZE),
            key_mask,
        )
        query_parts.append(query_grad.reshape(tokens, groups * HEAD_SIZE))
        key_parts.append(key_grad)
        value_parts.append(value_grad)
    query_out = jnp.concatenate(query_parts, 1).astype(jnp.bfloat16)
    key_grad = jnp.concatenate(key_parts, 1)
    value_grad = jnp.concatenate(value_parts, 1)
    memory_key_grad, local_key = (key_grad[:count], key_grad[count:])
    memory_value_grad, local_value = (value_grad[:count], value_grad[count:])
    back_key, back_value = (
        lax.psum_scatter(memory_key_grad, "ctx", scatter_dimension=0, tiled=True),
        lax.psum_scatter(memory_value_grad, "ctx", scatter_dimension=0, tiled=True),
    )
    key_out = (
        local_key + lax.dynamic_update_slice_in_dim(jnp.zeros_like(local_key), back_key, length, 0)
    ).astype(jnp.bfloat16)
    value_result = (
        local_value
        + lax.dynamic_update_slice_in_dim(jnp.zeros_like(local_value), back_value, length, 0)
    ).astype(jnp.bfloat16)
    low_rank_rows = jnp.dot(
        hidden_row_block, adapter_down_weight, preferred_element_type=jnp.float32
    ).astype(jnp.bfloat16)
    packed = adapter_terms(hidden_row_block, low_rank_rows, value_result, adapter_up_weight)
    packed = butterfly_sum(butterfly_sum(packed, "dp"), "ctx")
    model_width = hidden_row_block.shape[1]
    adapter_factor = adapter_scale / (log_batch * segment_list)
    down_sum = packed[:, :model_width].T
    up_sum = packed[:, model_width:]
    return (
        query_out[None, None],
        key_out[None, None],
        value_result[None, None],
        down_sum * adapter_factor,
        up_sum * adapter_factor,
    )


def solution(mesh):
    placed = (
        P("dp", "ctx", None, None),
        P("dp", "ctx", None, None),
        P("dp", "ctx", None, None),
        P("dp", "ctx", None, None),
        P("dp", "ctx", None, None),
        P(),
        P(),
        P("dp", "ctx"),
    )
    return jax.shard_map(
        per_device,
        mesh=mesh,
        in_specs=placed,
        out_specs=(
            P("dp", "ctx", None, None),
            P("dp", "ctx", None, None),
            P("dp", "ctx", None, None),
            P(),
            P(),
        ),
        check_vma=False,
    )
```

```python
import math

import jax
import jax.numpy as jnp
from jax import lax
from jax.sharding import PartitionSpec as P

HEAD_SIZE = 128
SUMM = 50


adapter_scale = 2.0


def group_grads(query_group, key_group, value_group, cot_group, key_mask):
    softmax_scale = 1.0 / math.sqrt(HEAD_SIZE)
    scores = (
        jnp.einsum("tgd,md->gtm", query_group, key_group, preferred_element_type=jnp.float32)
        * softmax_scale
    )
    unnorm = jnp.exp(jnp.where(key_mask[None], scores, -jnp.inf))
    attend = unnorm / jnp.sum(unnorm, -1, keepdims=True)
    attend_grad = jnp.einsum(
        "tgd,md->gtm", cot_group, value_group, preferred_element_type=jnp.float32
    )
    row_dot = jnp.sum(attend * attend_grad, -1, keepdims=True)
    dscore = (attend * (attend_grad - row_dot)).astype(jnp.bfloat16)
    attend_low = attend.astype(jnp.bfloat16)
    query_grad = (
        jnp.einsum("gtm,md->tgd", dscore, key_group, preferred_element_type=jnp.float32)
        * softmax_scale
    )
    key_grad = (
        jnp.einsum("gtm,tgd->md", dscore, query_group, preferred_element_type=jnp.float32)
        * softmax_scale
    )
    value_grad = jnp.einsum(
        "gtm,tgd->md", attend_low, cot_group, preferred_element_type=jnp.float32
    )
    return (query_grad, key_grad, value_grad)


def adapter_terms(hidden_piece, low_rank_piece, value_piece, adapter_up_weight):
    contract = (((0,), (0,)), ((), ()))
    backward_step = lax.dot_general(
        value_piece, adapter_up_weight, (((1,), (1,)), ((), ())), preferred_element_type=jnp.float32
    ).astype(jnp.bfloat16)
    down_part_t = lax.dot_general(
        backward_step, hidden_piece, contract, preferred_element_type=jnp.float32
    )
    up_part = lax.dot_general(
        low_rank_piece, value_piece, contract, preferred_element_type=jnp.float32
    )
    return jnp.concatenate([down_part_t, up_part], 1)


def butterfly_sum(x, axis):
    n = lax.axis_size(axis)
    if n & (n - 1):
        return lax.psum(x, axis)
    k = 1
    while k < n:
        x = x + lax.ppermute(x, axis, [(i, i ^ k) for i in range(n)])
        k *= 2
    return x


def per_device(
    queries,
    rotated_key_rows,
    values,
    cotangent,
    hidden,
    adapter_down_weight,
    adapter_up_weight,
    segment_text_length,
):
    query_rows = queries[0, 0]
    key_local = rotated_key_rows[0, 0]
    value_local = values[0, 0]
    cot_rows = cotangent[0, 0]
    hidden_row_block = hidden[0, 0]
    length = segment_text_length[0, 0]
    position = lax.axis_index("ctx")
    segment_list = lax.axis_size("ctx")
    log_batch = lax.axis_size("dp")
    tokens = query_rows.shape[0]
    width = key_local.shape[1]
    kv_heads = width // HEAD_SIZE
    groups = query_rows.shape[1] // width
    live = length + SUMM
    rows = jnp.arange(tokens)
    cot_rows = jnp.where((rows < live)[:, None], cot_rows, jnp.zeros_like(cot_rows))
    own_keys = lax.dynamic_slice_in_dim(key_local, length, SUMM, 0)
    own_values = lax.dynamic_slice_in_dim(value_local, length, SUMM, 0)
    own_summary = jnp.concatenate([own_keys, own_values], 0)
    held = own_summary[None]
    hop = 1
    while hop < segment_list:
        arrived = lax.ppermute(held, "ctx", [(i, i + hop) for i in range(segment_list - hop)])
        held = jnp.concatenate([held, arrived], 0)
        hop *= 2
    gathered = held.reshape(segment_list, 2, SUMM, width)
    memory_keys = gathered[:, 0].reshape(segment_list * SUMM, width)
    memory_values = gathered[:, 1].reshape(segment_list * SUMM, width)
    count = memory_keys.shape[0]
    memory_distance = jnp.arange(count) // SUMM
    memory_seen = (memory_distance >= 1) & (memory_distance <= position)
    local_mask = (rows[None, :] <= rows[:, None]) & (rows[None, :] < live)
    memory_mask = jnp.broadcast_to(memory_seen[None, :], (tokens, count))
    key_mask = jnp.concatenate([memory_mask, local_mask], axis=1)
    all_keys = jnp.concatenate([memory_keys, key_local], 0)
    all_values = jnp.concatenate([memory_values, value_local], 0)
    query_parts, key_parts, value_parts = ([], [], [])
    for group in range(kv_heads):
        qcols = slice(group * groups * HEAD_SIZE, (group + 1) * groups * HEAD_SIZE)
        kcols = slice(group * HEAD_SIZE, (group + 1) * HEAD_SIZE)
        query_grad, key_grad, value_grad = group_grads(
            query_rows[:, qcols].reshape(tokens, groups, HEAD_SIZE),
            all_keys[:, kcols],
            all_values[:, kcols],
            cot_rows[:, qcols].reshape(tokens, groups, HEAD_SIZE),
            key_mask,
        )
        query_parts.append(query_grad.reshape(tokens, groups * HEAD_SIZE))
        key_parts.append(key_grad)
        value_parts.append(value_grad)
    query_out = jnp.concatenate(query_parts, 1).astype(jnp.bfloat16)
    key_grad = jnp.concatenate(key_parts, 1)
    value_grad = jnp.concatenate(value_parts, 1)
    memory_key_grad, local_key = (key_grad[:count], key_grad[count:])
    memory_value_grad, local_value = (value_grad[:count], value_grad[count:])
    owed = jnp.stack(
        [
            memory_key_grad.reshape(segment_list, SUMM, width),
            memory_value_grad.reshape(segment_list, SUMM, width),
        ],
        1,
    )
    hop = segment_list // 2
    while hop >= 1:
        returned = lax.ppermute(owed[hop : 2 * hop], "ctx", [(i, i - hop) for i in range(hop, segment_list)])
        owed = owed[:hop] + returned
        hop //= 2
    back_key, back_value = owed[0, 0], owed[0, 1]
    key_out = (
        local_key + lax.dynamic_update_slice_in_dim(jnp.zeros_like(local_key), back_key, length, 0)
    ).astype(jnp.bfloat16)
    value_result = (
        local_value
        + lax.dynamic_update_slice_in_dim(jnp.zeros_like(local_value), back_value, length, 0)
    ).astype(jnp.bfloat16)
    low_rank_rows = jnp.dot(
        hidden_row_block, adapter_down_weight, preferred_element_type=jnp.float32
    ).astype(jnp.bfloat16)
    packed = adapter_terms(hidden_row_block, low_rank_rows, value_result, adapter_up_weight)
    packed = butterfly_sum(butterfly_sum(packed, "dp"), "ctx")
    model_width = hidden_row_block.shape[1]
    adapter_factor = adapter_scale / (log_batch * segment_list)
    down_sum = packed[:, :model_width].T
    up_sum = packed[:, model_width:]
    return (
        query_out[None, None],
        key_out[None, None],
        value_result[None, None],
        down_sum * adapter_factor,
        up_sum * adapter_factor,
    )


def solution(mesh):
    placed = (
        P("dp", "ctx", None, None),
        P("dp", "ctx", None, None),
        P("dp", "ctx", None, None),
        P("dp", "ctx", None, None),
        P("dp", "ctx", None, None),
        P(),
        P(),
        P("dp", "ctx"),
    )
    return jax.shard_map(
        per_device,
        mesh=mesh,
        in_specs=placed,
        out_specs=(
            P("dp", "ctx", None, None),
            P("dp", "ctx", None, None),
            P("dp", "ctx", None, None),
            P(),
            P(),
        ),
        check_vma=False,
    )
```

```python
import math

import jax
import jax.numpy as jnp
from jax import lax
from jax.sharding import PartitionSpec as P

HEAD_SIZE = 128
SUMM = 50


adapter_scale = 2.0


def group_grads(query_group, key_group, value_group, cot_group, key_mask):
    softmax_scale = 1.0 / math.sqrt(HEAD_SIZE)
    scores = (
        jnp.einsum("tgd,md->gtm", query_group, key_group, preferred_element_type=jnp.float32)
        * softmax_scale
    )
    unnorm = jnp.exp(jnp.where(key_mask[None], scores, -jnp.inf))
    attend = unnorm / jnp.sum(unnorm, -1, keepdims=True)
    attend_grad = jnp.einsum(
        "tgd,md->gtm", cot_group, value_group, preferred_element_type=jnp.float32
    )
    row_dot = jnp.sum(attend * attend_grad, -1, keepdims=True)
    dscore = (attend * (attend_grad - row_dot)).astype(jnp.bfloat16)
    attend_low = attend.astype(jnp.bfloat16)
    query_grad = (
        jnp.einsum("gtm,md->tgd", dscore, key_group, preferred_element_type=jnp.float32)
        * softmax_scale
    )
    key_grad = (
        jnp.einsum("gtm,tgd->md", dscore, query_group, preferred_element_type=jnp.float32)
        * softmax_scale
    )
    value_grad = jnp.einsum(
        "gtm,tgd->md", attend_low, cot_group, preferred_element_type=jnp.float32
    )
    return (query_grad, key_grad, value_grad)


def adapter_terms(hidden_piece, low_rank_piece, value_piece, adapter_up_weight):
    contract = (((0,), (0,)), ((), ()))
    backward_step = lax.dot_general(
        value_piece, adapter_up_weight, (((1,), (1,)), ((), ())), preferred_element_type=jnp.float32
    ).astype(jnp.bfloat16)
    down_part_t = lax.dot_general(
        backward_step, hidden_piece, contract, preferred_element_type=jnp.float32
    )
    up_part = lax.dot_general(
        low_rank_piece, value_piece, contract, preferred_element_type=jnp.float32
    )
    return jnp.concatenate([down_part_t, up_part], 1)


def butterfly_sum(x, axis):
    n = lax.axis_size(axis)
    if n & (n - 1):
        return lax.psum(x, axis)
    k = 1
    while k < n:
        x = x + lax.ppermute(x, axis, [(i, i ^ k) for i in range(n)])
        k *= 2
    return x


def per_device(
    queries,
    rotated_key_rows,
    values,
    cotangent,
    hidden,
    adapter_down_weight,
    adapter_up_weight,
    segment_text_length,
):
    query_rows = queries[0, 0]
    key_local = rotated_key_rows[0, 0]
    value_local = values[0, 0]
    cot_rows = cotangent[0, 0]
    hidden_row_block = hidden[0, 0]
    length = segment_text_length[0, 0]
    position = lax.axis_index("ctx")
    segment_list = lax.axis_size("ctx")
    log_batch = lax.axis_size("dp")
    tokens = query_rows.shape[0]
    width = key_local.shape[1]
    kv_heads = width // HEAD_SIZE
    groups = query_rows.shape[1] // width
    live = length + SUMM
    rows = jnp.arange(tokens)
    cot_rows = jnp.where((rows < live)[:, None], cot_rows, jnp.zeros_like(cot_rows))
    own_keys = lax.dynamic_slice_in_dim(key_local, length, SUMM, 0)
    own_values = lax.dynamic_slice_in_dim(value_local, length, SUMM, 0)
    own_summary = jnp.concatenate([own_keys, own_values], 0)
    held = own_summary[None]
    hop = 1
    while hop < segment_list:
        arrived = lax.ppermute(held, "ctx", [(i, i + hop) for i in range(segment_list - hop)])
        held = jnp.concatenate([held, arrived], 0)
        hop *= 2
    slot_of_segment = (position - jnp.arange(segment_list)) % segment_list
    gathered = jnp.take(held, slot_of_segment, axis=0).reshape(segment_list, 2, SUMM, width)
    memory_keys = gathered[:, 0].reshape(segment_list * SUMM, width)
    memory_values = gathered[:, 1].reshape(segment_list * SUMM, width)
    count = memory_keys.shape[0]
    memory_owner = jnp.arange(count) // SUMM
    local_mask = (rows[None, :] <= rows[:, None]) & (rows[None, :] < live)
    memory_mask = jnp.broadcast_to((memory_owner < position)[None, :], (tokens, count))
    key_mask = jnp.concatenate([memory_mask, local_mask], axis=1)
    all_keys = jnp.concatenate([memory_keys, key_local], 0)
    all_values = jnp.concatenate([memory_values, value_local], 0)
    query_parts, key_parts, value_parts = ([], [], [])
    for group in range(kv_heads):
        qcols = slice(group * groups * HEAD_SIZE, (group + 1) * groups * HEAD_SIZE)
        kcols = slice(group * HEAD_SIZE, (group + 1) * HEAD_SIZE)
        query_grad, key_grad, value_grad = group_grads(
            query_rows[:, qcols].reshape(tokens, groups, HEAD_SIZE),
            all_keys[:, kcols],
            all_values[:, kcols],
            cot_rows[:, qcols].reshape(tokens, groups, HEAD_SIZE),
            key_mask,
        )
        query_parts.append(query_grad.reshape(tokens, groups * HEAD_SIZE))
        key_parts.append(key_grad)
        value_parts.append(value_grad)
    query_out = jnp.concatenate(query_parts, 1).astype(jnp.bfloat16)
    key_grad = jnp.concatenate(key_parts, 1)
    value_grad = jnp.concatenate(value_parts, 1)
    memory_key_grad, local_key = (key_grad[:count], key_grad[count:])
    memory_value_grad, local_value = (value_grad[:count], value_grad[count:])
    back_key, back_value = (
        lax.psum_scatter(memory_key_grad, "ctx", scatter_dimension=0, tiled=True),
        lax.psum_scatter(memory_value_grad, "ctx", scatter_dimension=0, tiled=True),
    )
    key_out = (
        local_key + lax.dynamic_update_slice_in_dim(jnp.zeros_like(local_key), back_key, length, 0)
    ).astype(jnp.bfloat16)
    value_result = (
        local_value
        + lax.dynamic_update_slice_in_dim(jnp.zeros_like(local_value), back_value, length, 0)
    ).astype(jnp.bfloat16)
    low_rank_rows = jnp.dot(
        hidden_row_block, adapter_down_weight, preferred_element_type=jnp.float32
    ).astype(jnp.bfloat16)
    packed = adapter_terms(hidden_row_block, low_rank_rows, value_result, adapter_up_weight)
    packed = butterfly_sum(butterfly_sum(packed, "dp"), "ctx")
    model_width = hidden_row_block.shape[1]
    adapter_factor = adapter_scale / (log_batch * segment_list)
    down_sum = packed[:, :model_width].T
    up_sum = packed[:, model_width:]
    return (
        query_out[None, None],
        key_out[None, None],
        value_result[None, None],
        down_sum * adapter_factor,
        up_sum * adapter_factor,
    )


def solution(mesh):
    placed = (
        P("dp", "ctx", None, None),
        P("dp", "ctx", None, None),
        P("dp", "ctx", None, None),
        P("dp", "ctx", None, None),
        P("dp", "ctx", None, None),
        P(),
        P(),
        P("dp", "ctx"),
    )
    return jax.shard_map(
        per_device,
        mesh=mesh,
        in_specs=placed,
        out_specs=(
            P("dp", "ctx", None, None),
            P("dp", "ctx", None, None),
            P("dp", "ctx", None, None),
            P(),
            P(),
        ),
        check_vma=False,
    )
```

```python
import math

import jax
import numpy as np
import jax.numpy as jnp
from jax import lax
from jax.sharding import PartitionSpec as P

HEAD_SIZE = 128
SUMM = 50


adapter_scale = 2.0


def group_grads(query_group, key_group, value_group, cot_group, key_mask):
    softmax_scale = 1.0 / math.sqrt(HEAD_SIZE)
    scores = (
        jnp.einsum("tgd,md->gtm", query_group, key_group, preferred_element_type=jnp.float32)
        * softmax_scale
    )
    unnorm = jnp.exp(jnp.where(key_mask[None], scores, -jnp.inf))
    attend = unnorm / jnp.sum(unnorm, -1, keepdims=True)
    attend_grad = jnp.einsum(
        "tgd,md->gtm", cot_group, value_group, preferred_element_type=jnp.float32
    )
    row_dot = jnp.sum(attend * attend_grad, -1, keepdims=True)
    dscore = (attend * (attend_grad - row_dot)).astype(jnp.bfloat16)
    attend_low = attend.astype(jnp.bfloat16)
    query_grad = (
        jnp.einsum("gtm,md->tgd", dscore, key_group, preferred_element_type=jnp.float32)
        * softmax_scale
    )
    key_grad = (
        jnp.einsum("gtm,tgd->md", dscore, query_group, preferred_element_type=jnp.float32)
        * softmax_scale
    )
    value_grad = jnp.einsum(
        "gtm,tgd->md", attend_low, cot_group, preferred_element_type=jnp.float32
    )
    return (query_grad, key_grad, value_grad)


def adapter_terms(hidden_piece, low_rank_piece, value_piece, adapter_up_weight):
    contract = (((0,), (0,)), ((), ()))
    backward_step = lax.dot_general(
        value_piece, adapter_up_weight, (((1,), (1,)), ((), ())), preferred_element_type=jnp.float32
    ).astype(jnp.bfloat16)
    down_part_t = lax.dot_general(
        backward_step, hidden_piece, contract, preferred_element_type=jnp.float32
    )
    up_part = lax.dot_general(
        low_rank_piece, value_piece, contract, preferred_element_type=jnp.float32
    )
    return jnp.concatenate([down_part_t, up_part], 1)


def butterfly_sum(x, axis):
    n = lax.axis_size(axis)
    if n & (n - 1):
        return lax.psum(x, axis)
    k = 1
    while k < n:
        x = x + lax.ppermute(x, axis, [(i, i ^ k) for i in range(n)])
        k *= 2
    return x


def per_device(
    queries,
    rotated_key_rows,
    values,
    cotangent,
    hidden,
    adapter_down_weight,
    adapter_up_weight,
    segment_text_length,
):
    query_rows = queries[0, 0]
    key_local = rotated_key_rows[0, 0]
    value_local = values[0, 0]
    cot_rows = cotangent[0, 0]
    hidden_row_block = hidden[0, 0]
    length = segment_text_length[0, 0]
    position = lax.axis_index("ctx")
    segment_list = lax.axis_size("ctx")
    log_batch = lax.axis_size("dp")
    tokens = query_rows.shape[0]
    width = key_local.shape[1]
    kv_heads = width // HEAD_SIZE
    groups = query_rows.shape[1] // width
    live = length + SUMM
    rows = jnp.arange(tokens)
    cot_rows = jnp.where((rows < live)[:, None], cot_rows, jnp.zeros_like(cot_rows))
    own_keys = lax.dynamic_slice_in_dim(key_local, length, SUMM, 0)
    own_values = lax.dynamic_slice_in_dim(value_local, length, SUMM, 0)
    own_summary = jnp.concatenate([own_keys, own_values], 0)
    held = own_summary[None]
    distance_of_slot = [0]
    hop = segment_list // 2
    while hop >= 1:
        arrived = lax.ppermute(held, "ctx", [(i, i + hop) for i in range(segment_list - hop)])
        held = jnp.concatenate([held, arrived], 0)
        distance_of_slot = distance_of_slot + [d + hop for d in distance_of_slot]
        hop //= 2
    slot_of_distance = np.argsort(np.array(distance_of_slot)).astype(np.int32)
    slot_of_segment = jnp.asarray(slot_of_distance)[(position - jnp.arange(segment_list)) % segment_list]
    gathered = jnp.take(held, slot_of_segment, axis=0).reshape(segment_list, 2, SUMM, width)
    memory_keys = gathered[:, 0].reshape(segment_list * SUMM, width)
    memory_values = gathered[:, 1].reshape(segment_list * SUMM, width)
    count = memory_keys.shape[0]
    memory_owner = jnp.arange(count) // SUMM
    local_mask = (rows[None, :] <= rows[:, None]) & (rows[None, :] < live)
    memory_mask = jnp.broadcast_to((memory_owner < position)[None, :], (tokens, count))
    key_mask = jnp.concatenate([memory_mask, local_mask], axis=1)
    all_keys = jnp.concatenate([memory_keys, key_local], 0)
    all_values = jnp.concatenate([memory_values, value_local], 0)
    query_parts, key_parts, value_parts = ([], [], [])
    for group in range(kv_heads):
        qcols = slice(group * groups * HEAD_SIZE, (group + 1) * groups * HEAD_SIZE)
        kcols = slice(group * HEAD_SIZE, (group + 1) * HEAD_SIZE)
        query_grad, key_grad, value_grad = group_grads(
            query_rows[:, qcols].reshape(tokens, groups, HEAD_SIZE),
            all_keys[:, kcols],
            all_values[:, kcols],
            cot_rows[:, qcols].reshape(tokens, groups, HEAD_SIZE),
            key_mask,
        )
        query_parts.append(query_grad.reshape(tokens, groups * HEAD_SIZE))
        key_parts.append(key_grad)
        value_parts.append(value_grad)
    query_out = jnp.concatenate(query_parts, 1).astype(jnp.bfloat16)
    key_grad = jnp.concatenate(key_parts, 1)
    value_grad = jnp.concatenate(value_parts, 1)
    memory_key_grad, local_key = (key_grad[:count], key_grad[count:])
    memory_value_grad, local_value = (value_grad[:count], value_grad[count:])
    back_key, back_value = (
        lax.psum_scatter(memory_key_grad, "ctx", scatter_dimension=0, tiled=True),
        lax.psum_scatter(memory_value_grad, "ctx", scatter_dimension=0, tiled=True),
    )
    key_out = (
        local_key + lax.dynamic_update_slice_in_dim(jnp.zeros_like(local_key), back_key, length, 0)
    ).astype(jnp.bfloat16)
    value_result = (
        local_value
        + lax.dynamic_update_slice_in_dim(jnp.zeros_like(local_value), back_value, length, 0)
    ).astype(jnp.bfloat16)
    low_rank_rows = jnp.dot(
        hidden_row_block, adapter_down_weight, preferred_element_type=jnp.float32
    ).astype(jnp.bfloat16)
    packed = adapter_terms(hidden_row_block, low_rank_rows, value_result, adapter_up_weight)
    packed = butterfly_sum(butterfly_sum(packed, "dp"), "ctx")
    model_width = hidden_row_block.shape[1]
    adapter_factor = adapter_scale / (log_batch * segment_list)
    down_sum = packed[:, :model_width].T
    up_sum = packed[:, model_width:]
    return (
        query_out[None, None],
        key_out[None, None],
        value_result[None, None],
        down_sum * adapter_factor,
        up_sum * adapter_factor,
    )


def solution(mesh):
    placed = (
        P("dp", "ctx", None, None),
        P("dp", "ctx", None, None),
        P("dp", "ctx", None, None),
        P("dp", "ctx", None, None),
        P("dp", "ctx", None, None),
        P(),
        P(),
        P("dp", "ctx"),
    )
    return jax.shard_map(
        per_device,
        mesh=mesh,
        in_specs=placed,
        out_specs=(
            P("dp", "ctx", None, None),
            P("dp", "ctx", None, None),
            P("dp", "ctx", None, None),
            P(),
            P(),
        ),
        check_vma=False,
    )
```

```python
import math

import jax
import numpy as np
import jax.numpy as jnp
from jax import lax
from jax.sharding import PartitionSpec as P

HEAD_SIZE = 128
SUMM = 50


adapter_scale = 2.0


def group_grads(query_group, key_group, value_group, cot_group, key_mask):
    softmax_scale = 1.0 / math.sqrt(HEAD_SIZE)
    scores = (
        jnp.einsum("tgd,md->gtm", query_group, key_group, preferred_element_type=jnp.float32)
        * softmax_scale
    )
    unnorm = jnp.exp(jnp.where(key_mask[None], scores, -jnp.inf))
    attend = unnorm / jnp.sum(unnorm, -1, keepdims=True)
    attend_grad = jnp.einsum(
        "tgd,md->gtm", cot_group, value_group, preferred_element_type=jnp.float32
    )
    row_dot = jnp.sum(attend * attend_grad, -1, keepdims=True)
    dscore = (attend * (attend_grad - row_dot)).astype(jnp.bfloat16)
    attend_low = attend.astype(jnp.bfloat16)
    query_grad = (
        jnp.einsum("gtm,md->tgd", dscore, key_group, preferred_element_type=jnp.float32)
        * softmax_scale
    )
    key_grad = (
        jnp.einsum("gtm,tgd->md", dscore, query_group, preferred_element_type=jnp.float32)
        * softmax_scale
    )
    value_grad = jnp.einsum(
        "gtm,tgd->md", attend_low, cot_group, preferred_element_type=jnp.float32
    )
    return (query_grad, key_grad, value_grad)


def adapter_terms(hidden_piece, low_rank_piece, value_piece, adapter_up_weight):
    contract = (((0,), (0,)), ((), ()))
    backward_step = lax.dot_general(
        value_piece, adapter_up_weight, (((1,), (1,)), ((), ())), preferred_element_type=jnp.float32
    ).astype(jnp.bfloat16)
    down_part_t = lax.dot_general(
        backward_step, hidden_piece, contract, preferred_element_type=jnp.float32
    )
    up_part = lax.dot_general(
        low_rank_piece, value_piece, contract, preferred_element_type=jnp.float32
    )
    return jnp.concatenate([down_part_t, up_part], 1)


def butterfly_sum(x, axis):
    n = lax.axis_size(axis)
    if n & (n - 1):
        return lax.psum(x, axis)
    k = 1
    while k < n:
        x = x + lax.ppermute(x, axis, [(i, i ^ k) for i in range(n)])
        k *= 2
    return x


def exchange_pairs(axis, k):
    return [(i, i ^ k) for i in range(lax.axis_size(axis))]


def mesh_sum(x):
    n = lax.axis_size("dp")
    halving = [k for k in (1, 2) if k < n and not n & (n - 1)]
    if x.shape[-1] % (2 ** len(halving)):
        halving = []
    cur = x
    for k in halving:
        h = cur.shape[-1] // 2
        bit = (lax.axis_index("dp") // k) % 2
        keep = lax.dynamic_slice_in_dim(cur, bit * h, h, cur.ndim - 1)
        give = lax.dynamic_slice_in_dim(cur, (1 - bit) * h, h, cur.ndim - 1)
        cur = keep + lax.ppermute(give, "dp", exchange_pairs("dp", k))
    k = 2 ** len(halving)
    while k < n:
        cur = cur + lax.ppermute(cur, "dp", exchange_pairs("dp", k))
        k *= 2
    cur = butterfly_sum(cur, "ctx")
    for k in reversed(halving):
        bit = (lax.axis_index("dp") // k) % 2
        other = lax.ppermute(cur, "dp", exchange_pairs("dp", k))
        cur = jnp.where(
            bit == 0, jnp.concatenate([cur, other], -1), jnp.concatenate([other, cur], -1)
        )
    return cur


def per_device(
    queries,
    rotated_key_rows,
    values,
    cotangent,
    hidden,
    adapter_down_weight,
    adapter_up_weight,
    segment_text_length,
):
    query_rows = queries[0, 0]
    key_local = rotated_key_rows[0, 0]
    value_local = values[0, 0]
    cot_rows = cotangent[0, 0]
    hidden_row_block = hidden[0, 0]
    length = segment_text_length[0, 0]
    position = lax.axis_index("ctx")
    segment_list = lax.axis_size("ctx")
    log_batch = lax.axis_size("dp")
    tokens = query_rows.shape[0]
    width = key_local.shape[1]
    kv_heads = width // HEAD_SIZE
    groups = query_rows.shape[1] // width
    live = length + SUMM
    rows = jnp.arange(tokens)
    cot_rows = jnp.where((rows < live)[:, None], cot_rows, jnp.zeros_like(cot_rows))
    own_keys = lax.dynamic_slice_in_dim(key_local, length, SUMM, 0)
    own_values = lax.dynamic_slice_in_dim(value_local, length, SUMM, 0)
    own_summary = jnp.concatenate([own_keys, own_values], 0)
    held = own_summary[None]
    distance_of_slot = [0]
    hop = segment_list // 2
    while hop >= 1:
        arrived = lax.ppermute(held, "ctx", [(i, i + hop) for i in range(segment_list - hop)])
        held = jnp.concatenate([held, arrived], 0)
        distance_of_slot = distance_of_slot + [d + hop for d in distance_of_slot]
        hop //= 2
    slot_of_distance = np.argsort(np.array(distance_of_slot)).astype(np.int32)
    slot_of_segment = jnp.asarray(slot_of_distance)[(position - jnp.arange(segment_list)) % segment_list]
    gathered = jnp.take(held, slot_of_segment, axis=0).reshape(segment_list, 2, SUMM, width)
    memory_keys = gathered[:, 0].reshape(segment_list * SUMM, width)
    memory_values = gathered[:, 1].reshape(segment_list * SUMM, width)
    count = memory_keys.shape[0]
    memory_owner = jnp.arange(count) // SUMM
    local_mask = (rows[None, :] <= rows[:, None]) & (rows[None, :] < live)
    memory_mask = jnp.broadcast_to((memory_owner < position)[None, :], (tokens, count))
    key_mask = jnp.concatenate([memory_mask, local_mask], axis=1)
    all_keys = jnp.concatenate([memory_keys, key_local], 0)
    all_values = jnp.concatenate([memory_values, value_local], 0)
    query_parts, key_parts, value_parts = ([], [], [])
    for group in range(kv_heads):
        qcols = slice(group * groups * HEAD_SIZE, (group + 1) * groups * HEAD_SIZE)
        kcols = slice(group * HEAD_SIZE, (group + 1) * HEAD_SIZE)
        query_grad, key_grad, value_grad = group_grads(
            query_rows[:, qcols].reshape(tokens, groups, HEAD_SIZE),
            all_keys[:, kcols],
            all_values[:, kcols],
            cot_rows[:, qcols].reshape(tokens, groups, HEAD_SIZE),
            key_mask,
        )
        query_parts.append(query_grad.reshape(tokens, groups * HEAD_SIZE))
        key_parts.append(key_grad)
        value_parts.append(value_grad)
    query_out = jnp.concatenate(query_parts, 1).astype(jnp.bfloat16)
    key_grad = jnp.concatenate(key_parts, 1)
    value_grad = jnp.concatenate(value_parts, 1)
    memory_key_grad, local_key = (key_grad[:count], key_grad[count:])
    memory_value_grad, local_value = (value_grad[:count], value_grad[count:])
    back_key, back_value = (
        lax.psum_scatter(memory_key_grad, "ctx", scatter_dimension=0, tiled=True),
        lax.psum_scatter(memory_value_grad, "ctx", scatter_dimension=0, tiled=True),
    )
    key_out = (
        local_key + lax.dynamic_update_slice_in_dim(jnp.zeros_like(local_key), back_key, length, 0)
    ).astype(jnp.bfloat16)
    value_result = (
        local_value
        + lax.dynamic_update_slice_in_dim(jnp.zeros_like(local_value), back_value, length, 0)
    ).astype(jnp.bfloat16)
    low_rank_rows = jnp.dot(
        hidden_row_block, adapter_down_weight, preferred_element_type=jnp.float32
    ).astype(jnp.bfloat16)
    packed = adapter_terms(hidden_row_block, low_rank_rows, value_result, adapter_up_weight)
    packed = mesh_sum(packed)
    model_width = hidden_row_block.shape[1]
    adapter_factor = adapter_scale / (log_batch * segment_list)
    down_sum = packed[:, :model_width].T
    up_sum = packed[:, model_width:]
    return (
        query_out[None, None],
        key_out[None, None],
        value_result[None, None],
        down_sum * adapter_factor,
        up_sum * adapter_factor,
    )


def solution(mesh):
    placed = (
        P("dp", "ctx", None, None),
        P("dp", "ctx", None, None),
        P("dp", "ctx", None, None),
        P("dp", "ctx", None, None),
        P("dp", "ctx", None, None),
        P(),
        P(),
        P("dp", "ctx"),
    )
    return jax.shard_map(
        per_device,
        mesh=mesh,
        in_specs=placed,
        out_specs=(
            P("dp", "ctx", None, None),
            P("dp", "ctx", None, None),
            P("dp", "ctx", None, None),
            P(),
            P(),
        ),
        check_vma=False,
    )
```

```python
import math

import jax
import numpy as np
import jax.numpy as jnp
from jax import lax
from jax.sharding import PartitionSpec as P

HEAD_SIZE = 128
SUMM = 50


adapter_scale = 2.0


def group_grads(query_group, key_group, value_group, cot_group, key_mask):
    softmax_scale = 1.0 / math.sqrt(HEAD_SIZE)
    scores = (
        jnp.einsum("tgd,md->gtm", query_group, key_group, preferred_element_type=jnp.float32)
        * softmax_scale
    )
    unnorm = jnp.exp(jnp.where(key_mask[None], scores, -jnp.inf))
    attend = unnorm / jnp.sum(unnorm, -1, keepdims=True)
    attend_grad = jnp.einsum(
        "tgd,md->gtm", cot_group, value_group, preferred_element_type=jnp.float32
    )
    row_dot = jnp.sum(attend * attend_grad, -1, keepdims=True)
    dscore = (attend * (attend_grad - row_dot)).astype(jnp.bfloat16)
    attend_low = attend.astype(jnp.bfloat16)
    query_grad = (
        jnp.einsum("gtm,md->tgd", dscore, key_group, preferred_element_type=jnp.float32)
        * softmax_scale
    )
    key_grad = (
        jnp.einsum("gtm,tgd->md", dscore, query_group, preferred_element_type=jnp.float32)
        * softmax_scale
    )
    value_grad = jnp.einsum(
        "gtm,tgd->md", attend_low, cot_group, preferred_element_type=jnp.float32
    )
    return (query_grad, key_grad, value_grad)


def adapter_terms(hidden_piece, low_rank_piece, value_piece, adapter_up_weight):
    contract = (((0,), (0,)), ((), ()))
    backward_step = lax.dot_general(
        value_piece, adapter_up_weight, (((1,), (1,)), ((), ())), preferred_element_type=jnp.float32
    ).astype(jnp.bfloat16)
    down_part_t = lax.dot_general(
        backward_step, hidden_piece, contract, preferred_element_type=jnp.float32
    )
    up_part = lax.dot_general(
        low_rank_piece, value_piece, contract, preferred_element_type=jnp.float32
    )
    return jnp.concatenate([down_part_t, up_part], 1)


def butterfly_sum(x, axis):
    n = lax.axis_size(axis)
    if n & (n - 1):
        return lax.psum(x, axis)
    k = 1
    while k < n:
        x = x + lax.ppermute(x, axis, [(i, i ^ k) for i in range(n)])
        k *= 2
    return x


def exchange_pairs(axis, k):
    return [(i, i ^ k) for i in range(lax.axis_size(axis))]


def mesh_sum(x):
    n = lax.axis_size("dp")
    halving = [k for k in (1, 2) if k < n and not n & (n - 1)]
    if x.shape[-1] % (2 ** len(halving)):
        halving = []
    cur = x
    for k in halving:
        h = cur.shape[-1] // 2
        bit = (lax.axis_index("dp") // k) % 2
        keep = lax.dynamic_slice_in_dim(cur, bit * h, h, cur.ndim - 1)
        give = lax.dynamic_slice_in_dim(cur, (1 - bit) * h, h, cur.ndim - 1)
        cur = keep + lax.ppermute(give, "dp", exchange_pairs("dp", k))
    k = 2 ** len(halving)
    while k < n:
        cur = cur + lax.ppermute(cur, "dp", exchange_pairs("dp", k))
        k *= 2
    cur = butterfly_sum(cur, "ctx")
    for k in reversed(halving):
        bit = (lax.axis_index("dp") // k) % 2
        other = lax.ppermute(cur, "dp", exchange_pairs("dp", k))
        cur = jnp.where(
            bit == 0, jnp.concatenate([cur, other], -1), jnp.concatenate([other, cur], -1)
        )
    return cur


def per_device(
    queries,
    rotated_key_rows,
    values,
    cotangent,
    hidden,
    adapter_down_weight,
    adapter_up_weight,
    segment_text_length,
):
    query_rows = queries[0, 0]
    key_local = rotated_key_rows[0, 0]
    value_local = values[0, 0]
    cot_rows = cotangent[0, 0]
    hidden_row_block = hidden[0, 0]
    length = segment_text_length[0, 0]
    position = lax.axis_index("ctx")
    segment_list = lax.axis_size("ctx")
    log_batch = lax.axis_size("dp")
    tokens = query_rows.shape[0]
    width = key_local.shape[1]
    kv_heads = width // HEAD_SIZE
    groups = query_rows.shape[1] // width
    live = length + SUMM
    rows = jnp.arange(tokens)
    cot_rows = jnp.where((rows < live)[:, None], cot_rows, jnp.zeros_like(cot_rows))
    own_keys = lax.dynamic_slice_in_dim(key_local, length, SUMM, 0)
    own_values = lax.dynamic_slice_in_dim(value_local, length, SUMM, 0)
    own_summary = jnp.concatenate([own_keys, own_values], 0)
    held = own_summary[None]
    distance_of_slot = [0]
    hop = segment_list // 2
    while hop >= 1:
        arrived = lax.ppermute(held, "ctx", [(i, i + hop) for i in range(segment_list - hop)])
        held = jnp.concatenate([held, arrived], 0)
        distance_of_slot = distance_of_slot + [d + hop for d in distance_of_slot]
        hop //= 2
    slot_of_distance = np.argsort(np.array(distance_of_slot)).astype(np.int32)
    slot_of_segment = jnp.asarray(slot_of_distance)[(position - jnp.arange(segment_list)) % segment_list]
    gathered = jnp.take(held, slot_of_segment, axis=0).reshape(segment_list, 2, SUMM, width)
    memory_keys = gathered[:, 0].reshape(segment_list * SUMM, width)
    memory_values = gathered[:, 1].reshape(segment_list * SUMM, width)
    count = memory_keys.shape[0]
    memory_owner = jnp.arange(count) // SUMM
    local_mask = (rows[None, :] <= rows[:, None]) & (rows[None, :] < live)
    memory_mask = jnp.broadcast_to((memory_owner < position)[None, :], (tokens, count))
    key_mask = jnp.concatenate([memory_mask, local_mask], axis=1)
    all_keys = jnp.concatenate([memory_keys, key_local], 0)
    all_values = jnp.concatenate([memory_values, value_local], 0)
    query_parts, key_parts, value_parts = ([], [], [])
    for group in range(kv_heads):
        qcols = slice(group * groups * HEAD_SIZE, (group + 1) * groups * HEAD_SIZE)
        kcols = slice(group * HEAD_SIZE, (group + 1) * HEAD_SIZE)
        query_grad, key_grad, value_grad = group_grads(
            query_rows[:, qcols].reshape(tokens, groups, HEAD_SIZE),
            all_keys[:, kcols],
            all_values[:, kcols],
            cot_rows[:, qcols].reshape(tokens, groups, HEAD_SIZE),
            key_mask,
        )
        query_parts.append(query_grad.reshape(tokens, groups * HEAD_SIZE))
        key_parts.append(key_grad)
        value_parts.append(value_grad)
    query_out = jnp.concatenate(query_parts, 1).astype(jnp.bfloat16)
    key_grad = jnp.concatenate(key_parts, 1)
    value_grad = jnp.concatenate(value_parts, 1)
    memory_key_grad, local_key = (key_grad[:count], key_grad[count:])
    memory_value_grad, local_value = (value_grad[:count], value_grad[count:])
    segment_of_slot = (position - jnp.asarray(np.array(distance_of_slot, np.int32))) % segment_list
    owed = jnp.take(
        jnp.stack(
            [
                memory_key_grad.reshape(segment_list, SUMM, width),
                memory_value_grad.reshape(segment_list, SUMM, width),
            ],
            1,
        ),
        segment_of_slot,
        axis=0,
    )
    hop = 1
    while hop < segment_list:
        half = owed.shape[0] // 2
        returned = lax.ppermute(
            owed[half:], "ctx", [(i, i - hop) for i in range(hop, segment_list)]
        )
        owed = owed[:half] + returned
        hop *= 2
    back_key, back_value = owed[0, 0], owed[0, 1]
    key_out = (
        local_key + lax.dynamic_update_slice_in_dim(jnp.zeros_like(local_key), back_key, length, 0)
    ).astype(jnp.bfloat16)
    value_result = (
        local_value
        + lax.dynamic_update_slice_in_dim(jnp.zeros_like(local_value), back_value, length, 0)
    ).astype(jnp.bfloat16)
    low_rank_rows = jnp.dot(
        hidden_row_block, adapter_down_weight, preferred_element_type=jnp.float32
    ).astype(jnp.bfloat16)
    packed = adapter_terms(hidden_row_block, low_rank_rows, value_result, adapter_up_weight)
    packed = mesh_sum(packed)
    model_width = hidden_row_block.shape[1]
    adapter_factor = adapter_scale / (log_batch * segment_list)
    down_sum = packed[:, :model_width].T
    up_sum = packed[:, model_width:]
    return (
        query_out[None, None],
        key_out[None, None],
        value_result[None, None],
        down_sum * adapter_factor,
        up_sum * adapter_factor,
    )


def solution(mesh):
    placed = (
        P("dp", "ctx", None, None),
        P("dp", "ctx", None, None),
        P("dp", "ctx", None, None),
        P("dp", "ctx", None, None),
        P("dp", "ctx", None, None),
        P(),
        P(),
        P("dp", "ctx"),
    )
    return jax.shard_map(
        per_device,
        mesh=mesh,
        in_specs=placed,
        out_specs=(
            P("dp", "ctx", None, None),
            P("dp", "ctx", None, None),
            P("dp", "ctx", None, None),
            P(),
            P(),
        ),
        check_vma=False,
    )
```

```python
import math

import jax
import numpy as np
import jax.numpy as jnp
from jax import lax
from jax.sharding import PartitionSpec as P

HEAD_SIZE = 128
SUMM = 50


adapter_scale = 2.0


def group_grads(query_group, cot_group, parts):
    softmax_scale = 1.0 / math.sqrt(HEAD_SIZE)
    unnorms, attend_grads = [], []
    for key_part, value_part, mask_part in parts:
        scores = (
            jnp.einsum("tgd,md->gtm", query_group, key_part, preferred_element_type=jnp.float32)
            * softmax_scale
        )
        unnorms.append(jnp.exp(jnp.where(mask_part[None], scores, -jnp.inf)))
        attend_grads.append(
            jnp.einsum("tgd,md->gtm", cot_group, value_part, preferred_element_type=jnp.float32)
        )
    total = sum(jnp.sum(u, -1, keepdims=True) for u in unnorms)
    attends = [u / total for u in unnorms]
    row_dot = sum(
        jnp.sum(p * g, -1, keepdims=True) for p, g in zip(attends, attend_grads)
    )
    query_grad = None
    key_grads, value_grads = [], []
    for (key_part, _, _), attend, attend_grad in zip(parts, attends, attend_grads):
        dscore = (attend * (attend_grad - row_dot)).astype(jnp.bfloat16)
        attend_low = attend.astype(jnp.bfloat16)
        term = jnp.einsum("gtm,md->tgd", dscore, key_part, preferred_element_type=jnp.float32)
        query_grad = term if query_grad is None else query_grad + term
        key_grads.append(
            jnp.einsum("gtm,tgd->md", dscore, query_group, preferred_element_type=jnp.float32)
            * softmax_scale
        )
        value_grads.append(
            jnp.einsum("gtm,tgd->md", attend_low, cot_group, preferred_element_type=jnp.float32)
        )
    return (query_grad * softmax_scale, key_grads, value_grads)


def adapter_terms(hidden_piece, low_rank_piece, value_piece, adapter_up_weight):
    contract = (((0,), (0,)), ((), ()))
    backward_step = lax.dot_general(
        value_piece, adapter_up_weight, (((1,), (1,)), ((), ())), preferred_element_type=jnp.float32
    ).astype(jnp.bfloat16)
    down_part_t = lax.dot_general(
        backward_step, hidden_piece, contract, preferred_element_type=jnp.float32
    )
    up_part = lax.dot_general(
        low_rank_piece, value_piece, contract, preferred_element_type=jnp.float32
    )
    return jnp.concatenate([down_part_t, up_part], 1)


def butterfly_sum(x, axis):
    n = lax.axis_size(axis)
    if n & (n - 1):
        return lax.psum(x, axis)
    k = 1
    while k < n:
        x = x + lax.ppermute(x, axis, [(i, i ^ k) for i in range(n)])
        k *= 2
    return x


def exchange_pairs(axis, k):
    return [(i, i ^ k) for i in range(lax.axis_size(axis))]


def mesh_sum(x):
    n = lax.axis_size("dp")
    halving = [k for k in (1, 2) if k < n and not n & (n - 1)]
    if x.shape[-1] % (2 ** len(halving)):
        halving = []
    cur = x
    for k in halving:
        h = cur.shape[-1] // 2
        bit = (lax.axis_index("dp") // k) % 2
        keep = lax.dynamic_slice_in_dim(cur, bit * h, h, cur.ndim - 1)
        give = lax.dynamic_slice_in_dim(cur, (1 - bit) * h, h, cur.ndim - 1)
        cur = keep + lax.ppermute(give, "dp", exchange_pairs("dp", k))
    k = 2 ** len(halving)
    while k < n:
        cur = cur + lax.ppermute(cur, "dp", exchange_pairs("dp", k))
        k *= 2
    cur = butterfly_sum(cur, "ctx")
    for k in reversed(halving):
        bit = (lax.axis_index("dp") // k) % 2
        other = lax.ppermute(cur, "dp", exchange_pairs("dp", k))
        cur = jnp.where(
            bit == 0, jnp.concatenate([cur, other], -1), jnp.concatenate([other, cur], -1)
        )
    return cur


def per_device(
    queries,
    rotated_key_rows,
    values,
    cotangent,
    hidden,
    adapter_down_weight,
    adapter_up_weight,
    segment_text_length,
):
    query_rows = queries[0, 0]
    key_local = rotated_key_rows[0, 0]
    value_local = values[0, 0]
    cot_rows = cotangent[0, 0]
    hidden_row_block = hidden[0, 0]
    length = segment_text_length[0, 0]
    position = lax.axis_index("ctx")
    segment_list = lax.axis_size("ctx")
    log_batch = lax.axis_size("dp")
    tokens = query_rows.shape[0]
    width = key_local.shape[1]
    kv_heads = width // HEAD_SIZE
    groups = query_rows.shape[1] // width
    live = length + SUMM
    rows = jnp.arange(tokens)
    cot_rows = jnp.where((rows < live)[:, None], cot_rows, jnp.zeros_like(cot_rows))
    own_keys = lax.dynamic_slice_in_dim(key_local, length, SUMM, 0)
    own_values = lax.dynamic_slice_in_dim(value_local, length, SUMM, 0)
    own_summary = jnp.concatenate([own_keys, own_values], 0)
    held = own_summary[None]
    distance_of_slot = [0]
    hop = segment_list // 2
    while hop >= 1:
        arrived = lax.ppermute(held, "ctx", [(i, i + hop) for i in range(segment_list - hop)])
        held = jnp.concatenate([held, arrived], 0)
        distance_of_slot = distance_of_slot + [d + hop for d in distance_of_slot]
        hop //= 2
    slot_of_distance = np.argsort(np.array(distance_of_slot)).astype(np.int32)
    slot_of_segment = jnp.asarray(slot_of_distance)[(position - jnp.arange(segment_list)) % segment_list]
    gathered = jnp.take(held, slot_of_segment, axis=0).reshape(segment_list, 2, SUMM, width)
    memory_keys = gathered[:, 0].reshape(segment_list * SUMM, width)
    memory_values = gathered[:, 1].reshape(segment_list * SUMM, width)
    count = memory_keys.shape[0]
    memory_owner = jnp.arange(count) // SUMM
    local_mask = (rows[None, :] <= rows[:, None]) & (rows[None, :] < live)
    memory_mask = jnp.broadcast_to((memory_owner < position)[None, :], (tokens, count))
    query_parts, memory_key_parts, local_key_parts = ([], [], [])
    memory_value_parts, local_value_parts = ([], [])
    for group in range(kv_heads):
        qcols = slice(group * groups * HEAD_SIZE, (group + 1) * groups * HEAD_SIZE)
        kcols = slice(group * HEAD_SIZE, (group + 1) * HEAD_SIZE)
        query_grad, key_grads, value_grads = group_grads(
            query_rows[:, qcols].reshape(tokens, groups, HEAD_SIZE),
            cot_rows[:, qcols].reshape(tokens, groups, HEAD_SIZE),
            [
                (key_local[:, kcols], value_local[:, kcols], local_mask),
                (memory_keys[:, kcols], memory_values[:, kcols], memory_mask),
            ],
        )
        query_parts.append(query_grad.reshape(tokens, groups * HEAD_SIZE))
        local_key_parts.append(key_grads[0])
        memory_key_parts.append(key_grads[1])
        local_value_parts.append(value_grads[0])
        memory_value_parts.append(value_grads[1])
    query_out = jnp.concatenate(query_parts, 1).astype(jnp.bfloat16)
    memory_key_grad = jnp.concatenate(memory_key_parts, 1)
    local_key = jnp.concatenate(local_key_parts, 1)
    memory_value_grad = jnp.concatenate(memory_value_parts, 1)
    local_value = jnp.concatenate(local_value_parts, 1)
    back_key, back_value = (
        lax.psum_scatter(memory_key_grad, "ctx", scatter_dimension=0, tiled=True),
        lax.psum_scatter(memory_value_grad, "ctx", scatter_dimension=0, tiled=True),
    )
    key_out = (
        local_key + lax.dynamic_update_slice_in_dim(jnp.zeros_like(local_key), back_key, length, 0)
    ).astype(jnp.bfloat16)
    value_result = (
        local_value
        + lax.dynamic_update_slice_in_dim(jnp.zeros_like(local_value), back_value, length, 0)
    ).astype(jnp.bfloat16)
    low_rank_rows = jnp.dot(
        hidden_row_block, adapter_down_weight, preferred_element_type=jnp.float32
    ).astype(jnp.bfloat16)
    packed = adapter_terms(hidden_row_block, low_rank_rows, value_result, adapter_up_weight)
    packed = mesh_sum(packed)
    model_width = hidden_row_block.shape[1]
    adapter_factor = adapter_scale / (log_batch * segment_list)
    down_sum = packed[:, :model_width].T
    up_sum = packed[:, model_width:]
    return (
        query_out[None, None],
        key_out[None, None],
        value_result[None, None],
        down_sum * adapter_factor,
        up_sum * adapter_factor,
    )


def solution(mesh):
    placed = (
        P("dp", "ctx", None, None),
        P("dp", "ctx", None, None),
        P("dp", "ctx", None, None),
        P("dp", "ctx", None, None),
        P("dp", "ctx", None, None),
        P(),
        P(),
        P("dp", "ctx"),
    )
    return jax.shard_map(
        per_device,
        mesh=mesh,
        in_specs=placed,
        out_specs=(
            P("dp", "ctx", None, None),
            P("dp", "ctx", None, None),
            P("dp", "ctx", None, None),
            P(),
            P(),
        ),
        check_vma=False,
    )
```

```python
import math

import jax
import numpy as np
import jax.numpy as jnp
from jax import lax
from jax.sharding import PartitionSpec as P

HEAD_SIZE = 128
SUMM = 50


adapter_scale = 2.0


def group_grads(query_group, key_group, value_group, cot_group, key_mask):
    softmax_scale = 1.0 / math.sqrt(HEAD_SIZE)
    scores = (
        jnp.einsum("tgd,md->gtm", query_group, key_group, preferred_element_type=jnp.float32)
        * softmax_scale
    )
    unnorm = jnp.exp(jnp.where(key_mask[None], scores, -jnp.inf))
    attend = unnorm / jnp.sum(unnorm, -1, keepdims=True)
    attend_grad = jnp.einsum(
        "tgd,md->gtm", cot_group, value_group, preferred_element_type=jnp.float32
    )
    row_dot = jnp.sum(attend * attend_grad, -1, keepdims=True)
    dscore = (attend * (attend_grad - row_dot)).astype(jnp.bfloat16)
    attend_low = attend.astype(jnp.bfloat16)
    query_grad = (
        jnp.einsum("gtm,md->tgd", dscore, key_group, preferred_element_type=jnp.float32)
        * softmax_scale
    )
    key_grad = (
        jnp.einsum("gtm,tgd->md", dscore, query_group, preferred_element_type=jnp.float32)
        * softmax_scale
    )
    value_grad = jnp.einsum(
        "gtm,tgd->md", attend_low, cot_group, preferred_element_type=jnp.float32
    )
    return (query_grad, key_grad, value_grad)


def adapter_terms(hidden_piece, low_rank_piece, value_piece, adapter_up_weight):
    contract = (((0,), (0,)), ((), ()))
    backward_step = lax.dot_general(
        value_piece, adapter_up_weight, (((1,), (1,)), ((), ())), preferred_element_type=jnp.float32
    ).astype(jnp.bfloat16)
    down_part_t = lax.dot_general(
        backward_step, hidden_piece, contract, preferred_element_type=jnp.float32
    )
    up_part = lax.dot_general(
        low_rank_piece, value_piece, contract, preferred_element_type=jnp.float32
    )
    return jnp.concatenate([down_part_t, up_part], 1)


def butterfly_sum(x, axis):
    n = lax.axis_size(axis)
    if n & (n - 1):
        return lax.psum(x, axis)
    k = 1
    while k < n:
        x = x + lax.ppermute(x, axis, [(i, i ^ k) for i in range(n)])
        k *= 2
    return x


def exchange_pairs(axis, k):
    return [(i, i ^ k) for i in range(lax.axis_size(axis))]


def mesh_sum(x):
    n = lax.axis_size("dp")
    halving = [k for k in (1, 2) if k < n and not n & (n - 1)]
    if x.shape[-1] % (2 ** len(halving)):
        halving = []
    cur = x
    for k in halving:
        h = cur.shape[-1] // 2
        bit = (lax.axis_index("dp") // k) % 2
        keep = lax.dynamic_slice_in_dim(cur, bit * h, h, cur.ndim - 1)
        give = lax.dynamic_slice_in_dim(cur, (1 - bit) * h, h, cur.ndim - 1)
        cur = keep + lax.ppermute(give, "dp", exchange_pairs("dp", k))
    k = 2 ** len(halving)
    while k < n:
        cur = cur + lax.ppermute(cur, "dp", exchange_pairs("dp", k))
        k *= 2
    cur = butterfly_sum(cur, "ctx")
    for k in reversed(halving):
        bit = (lax.axis_index("dp") // k) % 2
        other = lax.ppermute(cur, "dp", exchange_pairs("dp", k))
        cur = jnp.where(
            bit == 0, jnp.concatenate([cur, other], -1), jnp.concatenate([other, cur], -1)
        )
    return cur


def per_device(
    queries,
    rotated_key_rows,
    values,
    cotangent,
    hidden,
    adapter_down_weight,
    adapter_up_weight,
    segment_text_length,
):
    query_rows = queries[0, 0]
    key_local = rotated_key_rows[0, 0]
    value_local = values[0, 0]
    cot_rows = cotangent[0, 0]
    hidden_row_block = hidden[0, 0]
    length = segment_text_length[0, 0]
    position = lax.axis_index("ctx")
    segment_list = lax.axis_size("ctx")
    log_batch = lax.axis_size("dp")
    tokens = query_rows.shape[0]
    width = key_local.shape[1]
    kv_heads = width // HEAD_SIZE
    groups = query_rows.shape[1] // width
    live = length + SUMM
    rows = jnp.arange(tokens)
    cot_rows = jnp.where((rows < live)[:, None], cot_rows, jnp.zeros_like(cot_rows))
    own_keys = lax.dynamic_slice_in_dim(key_local, length, SUMM, 0)
    own_values = lax.dynamic_slice_in_dim(value_local, length, SUMM, 0)
    own_summary = jnp.concatenate([own_keys, own_values], 0)
    held = own_summary[None]
    distance_of_slot = [0]
    hop = segment_list // 2
    while hop >= 1:
        arrived = lax.ppermute(held, "ctx", [(i, i + hop) for i in range(segment_list - hop)])
        held = jnp.concatenate([held, arrived], 0)
        distance_of_slot = distance_of_slot + [d + hop for d in distance_of_slot]
        hop //= 2
    slot_of_distance = np.argsort(np.array(distance_of_slot)).astype(np.int32)
    slot_of_segment = jnp.asarray(slot_of_distance)[(position - jnp.arange(segment_list)) % segment_list]
    gathered = jnp.take(held, slot_of_segment, axis=0).reshape(segment_list, 2, SUMM, width)
    memory_keys = gathered[:, 0].reshape(segment_list * SUMM, width)
    memory_values = gathered[:, 1].reshape(segment_list * SUMM, width)
    count = memory_keys.shape[0]
    memory_owner = jnp.arange(count) // SUMM
    local_mask = (rows[None, :] <= rows[:, None]) & (rows[None, :] < live)
    memory_mask = jnp.broadcast_to((memory_owner < position)[None, :], (tokens, count))
    key_mask = jnp.concatenate([memory_mask, local_mask], axis=1)
    all_keys = jnp.concatenate([memory_keys, key_local], 0)
    all_values = jnp.concatenate([memory_values, value_local], 0)
    softmax_scale = 1.0 / math.sqrt(HEAD_SIZE)
    query_heads = query_rows.reshape(tokens, kv_heads, groups, HEAD_SIZE)
    cot_heads = cot_rows.reshape(tokens, kv_heads, groups, HEAD_SIZE)
    key_heads = all_keys.reshape(-1, kv_heads, HEAD_SIZE)
    value_heads = all_values.reshape(-1, kv_heads, HEAD_SIZE)
    scores = (
        jnp.einsum("tkgd,mkd->kgtm", query_heads, key_heads, preferred_element_type=jnp.float32)
        * softmax_scale
    )
    unnorm = jnp.exp(jnp.where(key_mask[None, None], scores, -jnp.inf))
    attend = unnorm / jnp.sum(unnorm, -1, keepdims=True)
    attend_grad = jnp.einsum(
        "tkgd,mkd->kgtm", cot_heads, value_heads, preferred_element_type=jnp.float32
    )
    row_dot = jnp.sum(attend * attend_grad, -1, keepdims=True)
    dscore = (attend * (attend_grad - row_dot)).astype(jnp.bfloat16)
    attend_low = attend.astype(jnp.bfloat16)
    query_out = (
        jnp.einsum("kgtm,mkd->tkgd", dscore, key_heads, preferred_element_type=jnp.float32)
        * softmax_scale
    ).reshape(tokens, kv_heads * groups * HEAD_SIZE).astype(jnp.bfloat16)
    key_grad = (
        jnp.einsum("kgtm,tkgd->mkd", dscore, query_heads, preferred_element_type=jnp.float32)
        * softmax_scale
    )
    value_grad = jnp.einsum(
        "kgtm,tkgd->mkd", attend_low, cot_heads, preferred_element_type=jnp.float32
    )
    key_grad = jnp.concatenate([key_grad[:, h] for h in range(kv_heads)], 1)
    value_grad = jnp.concatenate([value_grad[:, h] for h in range(kv_heads)], 1)
    memory_key_grad, local_key = (key_grad[:count], key_grad[count:])
    memory_value_grad, local_value = (value_grad[:count], value_grad[count:])
    back_key, back_value = (
        lax.psum_scatter(memory_key_grad, "ctx", scatter_dimension=0, tiled=True),
        lax.psum_scatter(memory_value_grad, "ctx", scatter_dimension=0, tiled=True),
    )
    key_out = (
        local_key + lax.dynamic_update_slice_in_dim(jnp.zeros_like(local_key), back_key, length, 0)
    ).astype(jnp.bfloat16)
    value_result = (
        local_value
        + lax.dynamic_update_slice_in_dim(jnp.zeros_like(local_value), back_value, length, 0)
    ).astype(jnp.bfloat16)
    low_rank_rows = jnp.dot(
        hidden_row_block, adapter_down_weight, preferred_element_type=jnp.float32
    ).astype(jnp.bfloat16)
    packed = adapter_terms(hidden_row_block, low_rank_rows, value_result, adapter_up_weight)
    packed = mesh_sum(packed)
    model_width = hidden_row_block.shape[1]
    adapter_factor = adapter_scale / (log_batch * segment_list)
    down_sum = packed[:, :model_width].T
    up_sum = packed[:, model_width:]
    return (
        query_out[None, None],
        key_out[None, None],
        value_result[None, None],
        down_sum * adapter_factor,
        up_sum * adapter_factor,
    )


def solution(mesh):
    placed = (
        P("dp", "ctx", None, None),
        P("dp", "ctx", None, None),
        P("dp", "ctx", None, None),
        P("dp", "ctx", None, None),
        P("dp", "ctx", None, None),
        P(),
        P(),
        P("dp", "ctx"),
    )
    return jax.shard_map(
        per_device,
        mesh=mesh,
        in_specs=placed,
        out_specs=(
            P("dp", "ctx", None, None),
            P("dp", "ctx", None, None),
            P("dp", "ctx", None, None),
            P(),
            P(),
        ),
        check_vma=False,
    )
```

```python
import math

import jax
import numpy as np
import jax.numpy as jnp
from jax import lax
from jax.sharding import PartitionSpec as P

HEAD_SIZE = 128
SUMM = 50


adapter_scale = 2.0


def group_grads(query_group, key_group, value_group, cot_group, key_mask):
    softmax_scale = 1.0 / math.sqrt(HEAD_SIZE)
    scores = (
        jnp.einsum("tgd,md->gtm", query_group, key_group, preferred_element_type=jnp.float32)
        * softmax_scale
    )
    unnorm = jnp.exp(jnp.where(key_mask[None], scores, -jnp.inf))
    attend = unnorm / jnp.sum(unnorm, -1, keepdims=True)
    attend_grad = jnp.einsum(
        "tgd,md->gtm", cot_group, value_group, preferred_element_type=jnp.float32
    )
    row_dot = jnp.sum(attend * attend_grad, -1, keepdims=True)
    dscore = (attend * (attend_grad - row_dot)).astype(jnp.bfloat16)
    attend_low = attend.astype(jnp.bfloat16)
    query_grad = (
        jnp.einsum("gtm,md->tgd", dscore, key_group, preferred_element_type=jnp.float32)
        * softmax_scale
    )
    key_grad = (
        jnp.einsum("gtm,tgd->md", dscore, query_group, preferred_element_type=jnp.float32)
        * softmax_scale
    )
    value_grad = jnp.einsum(
        "gtm,tgd->md", attend_low, cot_group, preferred_element_type=jnp.float32
    )
    return (query_grad, key_grad, value_grad)


def adapter_terms(hidden_piece, low_rank_piece, value_piece, adapter_up_weight):
    contract = (((0,), (0,)), ((), ()))
    backward_step = lax.dot_general(
        value_piece, adapter_up_weight, (((1,), (1,)), ((), ())), preferred_element_type=jnp.float32
    ).astype(jnp.bfloat16)
    down_part_t = lax.dot_general(
        backward_step, hidden_piece, contract, preferred_element_type=jnp.float32
    )
    up_part = lax.dot_general(
        low_rank_piece, value_piece, contract, preferred_element_type=jnp.float32
    )
    return jnp.concatenate([down_part_t, up_part], 1)


def butterfly_sum(x, axis):
    n = lax.axis_size(axis)
    if n & (n - 1):
        return lax.psum(x, axis)
    k = 1
    while k < n:
        x = x + lax.ppermute(x, axis, [(i, i ^ k) for i in range(n)])
        k *= 2
    return x


def exchange_pairs(axis, k):
    return [(i, i ^ k) for i in range(lax.axis_size(axis))]


def mesh_sum(x):
    n = lax.axis_size("dp")
    halving = [k for k in (1, 2) if k < n and not n & (n - 1)]
    if x.shape[-1] % (2 ** len(halving)):
        halving = []
    cur = x
    for k in halving:
        h = cur.shape[-1] // 2
        bit = (lax.axis_index("dp") // k) % 2
        keep = lax.dynamic_slice_in_dim(cur, bit * h, h, cur.ndim - 1)
        give = lax.dynamic_slice_in_dim(cur, (1 - bit) * h, h, cur.ndim - 1)
        cur = keep + lax.ppermute(give, "dp", exchange_pairs("dp", k))
    k = 2 ** len(halving)
    while k < n:
        cur = cur + lax.ppermute(cur, "dp", exchange_pairs("dp", k))
        k *= 2
    cur = butterfly_sum(cur, "ctx")
    for k in reversed(halving):
        bit = (lax.axis_index("dp") // k) % 2
        other = lax.ppermute(cur, "dp", exchange_pairs("dp", k))
        cur = jnp.where(
            bit == 0, jnp.concatenate([cur, other], -1), jnp.concatenate([other, cur], -1)
        )
    return cur


def per_device(
    queries,
    rotated_key_rows,
    values,
    cotangent,
    hidden,
    adapter_down_weight,
    adapter_up_weight,
    segment_text_length,
):
    query_rows = queries[0, 0]
    key_local = rotated_key_rows[0, 0]
    value_local = values[0, 0]
    cot_rows = cotangent[0, 0]
    hidden_row_block = hidden[0, 0]
    length = segment_text_length[0, 0]
    position = lax.axis_index("ctx")
    segment_list = lax.axis_size("ctx")
    log_batch = lax.axis_size("dp")
    tokens = query_rows.shape[0]
    width = key_local.shape[1]
    kv_heads = width // HEAD_SIZE
    groups = query_rows.shape[1] // width
    live = length + SUMM
    rows = jnp.arange(tokens)
    cot_rows = jnp.where((rows < live)[:, None], cot_rows, jnp.zeros_like(cot_rows))
    own_keys = lax.dynamic_slice_in_dim(key_local, length, SUMM, 0)
    own_values = lax.dynamic_slice_in_dim(value_local, length, SUMM, 0)
    own_summary = jnp.concatenate([own_keys, own_values], 0)
    held = own_summary[None]
    distance_of_slot = [0]
    hop = segment_list // 2
    while hop >= 1:
        arrived = lax.ppermute(held, "ctx", [(i, i + hop) for i in range(segment_list - hop)])
        held = jnp.concatenate([held, arrived], 0)
        distance_of_slot = distance_of_slot + [d + hop for d in distance_of_slot]
        hop //= 2
    slot_of_distance = np.argsort(np.array(distance_of_slot)).astype(np.int32)
    slot_of_segment = jnp.asarray(slot_of_distance)[(position - jnp.arange(segment_list)) % segment_list]
    gathered = jnp.take(held, slot_of_segment, axis=0).reshape(segment_list, 2, SUMM, width)
    memory_keys = gathered[:, 0].reshape(segment_list * SUMM, width)
    memory_values = gathered[:, 1].reshape(segment_list * SUMM, width)
    count = memory_keys.shape[0]
    memory_owner = jnp.arange(count) // SUMM
    local_mask = (rows[None, :] <= rows[:, None]) & (rows[None, :] < live)
    memory_mask = jnp.broadcast_to((memory_owner < position)[None, :], (tokens, count))
    key_mask = jnp.concatenate([memory_mask, local_mask], axis=1)
    all_keys = jnp.concatenate([memory_keys, key_local], 0)
    all_values = jnp.concatenate([memory_values, value_local], 0)
    softmax_scale = 1.0 / math.sqrt(HEAD_SIZE)
    query_heads = query_rows.reshape(tokens, kv_heads, groups, HEAD_SIZE)
    cot_heads = cot_rows.reshape(tokens, kv_heads, groups, HEAD_SIZE)
    key_heads = all_keys.reshape(-1, kv_heads, HEAD_SIZE)
    value_heads = all_values.reshape(-1, kv_heads, HEAD_SIZE)
    scores = (
        jnp.einsum("tkgd,mkd->kgtm", query_heads, key_heads, preferred_element_type=jnp.float32)
        * softmax_scale
    )
    unnorm = jnp.exp(jnp.where(key_mask[None, None], scores, -jnp.inf))
    attend = unnorm / jnp.sum(unnorm, -1, keepdims=True)
    attend_grad = jnp.einsum(
        "tkgd,mkd->kgtm", cot_heads, value_heads, preferred_element_type=jnp.float32
    )
    row_dot = jnp.sum(attend * attend_grad, -1, keepdims=True)
    dscore = (attend * (attend_grad - row_dot)).astype(jnp.bfloat16)
    attend_low = attend.astype(jnp.bfloat16)
    query_out = (
        jnp.einsum("kgtm,mkd->tkgd", dscore, key_heads, preferred_element_type=jnp.float32)
        * softmax_scale
    ).reshape(tokens, kv_heads * groups * HEAD_SIZE).astype(jnp.bfloat16)
    key_grad = (
        jnp.einsum("kgtm,tkgd->mkd", dscore, query_heads, preferred_element_type=jnp.float32)
        * softmax_scale
    )
    value_grad = jnp.einsum(
        "kgtm,tkgd->mkd", attend_low, cot_heads, preferred_element_type=jnp.float32
    )
    key_grad = jnp.concatenate([key_grad[:, h] for h in range(kv_heads)], 1)
    value_grad = jnp.concatenate([value_grad[:, h] for h in range(kv_heads)], 1)
    memory_key_grad, local_key = (key_grad[:count], key_grad[count:])
    memory_value_grad, local_value = (value_grad[:count], value_grad[count:])
    back_value = lax.psum_scatter(memory_value_grad, "ctx", scatter_dimension=0, tiled=True)
    memory_key_grad, _ = lax.optimization_barrier((memory_key_grad, back_value))
    back_key = lax.psum_scatter(memory_key_grad, "ctx", scatter_dimension=0, tiled=True)
    key_out = (
        local_key + lax.dynamic_update_slice_in_dim(jnp.zeros_like(local_key), back_key, length, 0)
    ).astype(jnp.bfloat16)
    value_result = (
        local_value
        + lax.dynamic_update_slice_in_dim(jnp.zeros_like(local_value), back_value, length, 0)
    ).astype(jnp.bfloat16)
    low_rank_rows = jnp.dot(
        hidden_row_block, adapter_down_weight, preferred_element_type=jnp.float32
    ).astype(jnp.bfloat16)
    packed = adapter_terms(hidden_row_block, low_rank_rows, value_result, adapter_up_weight)
    packed = mesh_sum(packed)
    model_width = hidden_row_block.shape[1]
    adapter_factor = adapter_scale / (log_batch * segment_list)
    down_sum = packed[:, :model_width].T
    up_sum = packed[:, model_width:]
    return (
        query_out[None, None],
        key_out[None, None],
        value_result[None, None],
        down_sum * adapter_factor,
        up_sum * adapter_factor,
    )


def solution(mesh):
    placed = (
        P("dp", "ctx", None, None),
        P("dp", "ctx", None, None),
        P("dp", "ctx", None, None),
        P("dp", "ctx", None, None),
        P("dp", "ctx", None, None),
        P(),
        P(),
        P("dp", "ctx"),
    )
    return jax.shard_map(
        per_device,
        mesh=mesh,
        in_specs=placed,
        out_specs=(
            P("dp", "ctx", None, None),
            P("dp", "ctx", None, None),
            P("dp", "ctx", None, None),
            P(),
            P(),
        ),
        check_vma=False,
    )
```

```python
import math

import jax
import numpy as np
import jax.numpy as jnp
from jax import lax
from jax.sharding import PartitionSpec as P

HEAD_SIZE = 128
SUMM = 50


adapter_scale = 2.0


def group_grads(query_group, key_group, value_group, cot_group, key_mask):
    softmax_scale = 1.0 / math.sqrt(HEAD_SIZE)
    scores = (
        jnp.einsum("tgd,md->gtm", query_group, key_group, preferred_element_type=jnp.float32)
        * softmax_scale
    )
    unnorm = jnp.exp(jnp.where(key_mask[None], scores, -jnp.inf))
    attend = unnorm / jnp.sum(unnorm, -1, keepdims=True)
    attend_grad = jnp.einsum(
        "tgd,md->gtm", cot_group, value_group, preferred_element_type=jnp.float32
    )
    row_dot = jnp.sum(attend * attend_grad, -1, keepdims=True)
    dscore = (attend * (attend_grad - row_dot)).astype(jnp.bfloat16)
    attend_low = attend.astype(jnp.bfloat16)
    query_grad = (
        jnp.einsum("gtm,md->tgd", dscore, key_group, preferred_element_type=jnp.float32)
        * softmax_scale
    )
    key_grad = (
        jnp.einsum("gtm,tgd->md", dscore, query_group, preferred_element_type=jnp.float32)
        * softmax_scale
    )
    value_grad = jnp.einsum(
        "gtm,tgd->md", attend_low, cot_group, preferred_element_type=jnp.float32
    )
    return (query_grad, key_grad, value_grad)


def adapter_terms(hidden_piece, low_rank_piece, value_piece, adapter_up_weight):
    contract = (((0,), (0,)), ((), ()))
    backward_step = lax.dot_general(
        value_piece, adapter_up_weight, (((1,), (1,)), ((), ())), preferred_element_type=jnp.float32
    ).astype(jnp.bfloat16)
    down_part_t = lax.dot_general(
        backward_step, hidden_piece, contract, preferred_element_type=jnp.float32
    )
    up_part = lax.dot_general(
        low_rank_piece, value_piece, contract, preferred_element_type=jnp.float32
    )
    return jnp.concatenate([down_part_t, up_part], 1)


def butterfly_sum(x, axis):
    n = lax.axis_size(axis)
    if n & (n - 1):
        return lax.psum(x, axis)
    k = 1
    while k < n:
        x = x + lax.ppermute(x, axis, [(i, i ^ k) for i in range(n)])
        k *= 2
    return x


def exchange_pairs(axis, k):
    return [(i, i ^ k) for i in range(lax.axis_size(axis))]


def mesh_sum(x):
    rounds = []
    for axis in ("dp", "ctx"):
        n = lax.axis_size(axis)
        if n & (n - 1):
            return lax.psum(x, ("dp", "ctx"))
        rounds += [(axis, 1 << j) for j in range(n.bit_length() - 1)]
    nearest = [r for r in (("dp", 1), ("dp", 2), ("ctx", 1)) if r in rounds]
    halving = [r for r in nearest if x.shape[-1] % (2 ** len(nearest)) == 0]
    cur = x
    for axis, k in halving:
        h = cur.shape[-1] // 2
        bit = (lax.axis_index(axis) // k) % 2
        keep = lax.dynamic_slice_in_dim(cur, bit * h, h, cur.ndim - 1)
        give = lax.dynamic_slice_in_dim(cur, (1 - bit) * h, h, cur.ndim - 1)
        cur = keep + lax.ppermute(give, axis, exchange_pairs(axis, k))
    for axis, k in rounds:
        if (axis, k) not in halving:
            cur = cur + lax.ppermute(cur, axis, exchange_pairs(axis, k))
    for axis, k in reversed(halving):
        bit = (lax.axis_index(axis) // k) % 2
        other = lax.ppermute(cur, axis, exchange_pairs(axis, k))
        cur = jnp.where(
            bit == 0, jnp.concatenate([cur, other], -1), jnp.concatenate([other, cur], -1)
        )
    return cur


def per_device(
    queries,
    rotated_key_rows,
    values,
    cotangent,
    hidden,
    adapter_down_weight,
    adapter_up_weight,
    segment_text_length,
):
    query_rows = queries[0, 0]
    key_local = rotated_key_rows[0, 0]
    value_local = values[0, 0]
    cot_rows = cotangent[0, 0]
    hidden_row_block = hidden[0, 0]
    length = segment_text_length[0, 0]
    position = lax.axis_index("ctx")
    segment_list = lax.axis_size("ctx")
    log_batch = lax.axis_size("dp")
    tokens = query_rows.shape[0]
    width = key_local.shape[1]
    kv_heads = width // HEAD_SIZE
    groups = query_rows.shape[1] // width
    live = length + SUMM
    rows = jnp.arange(tokens)
    cot_rows = jnp.where((rows < live)[:, None], cot_rows, jnp.zeros_like(cot_rows))
    own_keys = lax.dynamic_slice_in_dim(key_local, length, SUMM, 0)
    own_values = lax.dynamic_slice_in_dim(value_local, length, SUMM, 0)
    own_summary = jnp.concatenate([own_keys, own_values], 0)
    held = own_summary[None]
    distance_of_slot = [0]
    hop = segment_list // 2
    while hop >= 1:
        arrived = lax.ppermute(held, "ctx", [(i, i + hop) for i in range(segment_list - hop)])
        held = jnp.concatenate([held, arrived], 0)
        distance_of_slot = distance_of_slot + [d + hop for d in distance_of_slot]
        hop //= 2
    slot_of_distance = np.argsort(np.array(distance_of_slot)).astype(np.int32)
    slot_of_segment = jnp.asarray(slot_of_distance)[(position - jnp.arange(segment_list)) % segment_list]
    gathered = jnp.take(held, slot_of_segment, axis=0).reshape(segment_list, 2, SUMM, width)
    memory_keys = gathered[:, 0].reshape(segment_list * SUMM, width)
    memory_values = gathered[:, 1].reshape(segment_list * SUMM, width)
    count = memory_keys.shape[0]
    memory_owner = jnp.arange(count) // SUMM
    local_mask = (rows[None, :] <= rows[:, None]) & (rows[None, :] < live)
    memory_mask = jnp.broadcast_to((memory_owner < position)[None, :], (tokens, count))
    key_mask = jnp.concatenate([memory_mask, local_mask], axis=1)
    all_keys = jnp.concatenate([memory_keys, key_local], 0)
    all_values = jnp.concatenate([memory_values, value_local], 0)
    softmax_scale = 1.0 / math.sqrt(HEAD_SIZE)
    query_heads = query_rows.reshape(tokens, kv_heads, groups, HEAD_SIZE)
    cot_heads = cot_rows.reshape(tokens, kv_heads, groups, HEAD_SIZE)
    key_heads = all_keys.reshape(-1, kv_heads, HEAD_SIZE)
    value_heads = all_values.reshape(-1, kv_heads, HEAD_SIZE)
    scores = (
        jnp.einsum("tkgd,mkd->kgtm", query_heads, key_heads, preferred_element_type=jnp.float32)
        * softmax_scale
    )
    unnorm = jnp.exp(jnp.where(key_mask[None, None], scores, -jnp.inf))
    attend = unnorm / jnp.sum(unnorm, -1, keepdims=True)
    attend_grad = jnp.einsum(
        "tkgd,mkd->kgtm", cot_heads, value_heads, preferred_element_type=jnp.float32
    )
    row_dot = jnp.sum(attend * attend_grad, -1, keepdims=True)
    dscore = (attend * (attend_grad - row_dot)).astype(jnp.bfloat16)
    attend_low = attend.astype(jnp.bfloat16)
    query_out = (
        jnp.einsum("kgtm,mkd->tkgd", dscore, key_heads, preferred_element_type=jnp.float32)
        * softmax_scale
    ).reshape(tokens, kv_heads * groups * HEAD_SIZE).astype(jnp.bfloat16)
    key_grad = (
        jnp.einsum("kgtm,tkgd->mkd", dscore, query_heads, preferred_element_type=jnp.float32)
        * softmax_scale
    )
    value_grad = jnp.einsum(
        "kgtm,tkgd->mkd", attend_low, cot_heads, preferred_element_type=jnp.float32
    )
    key_grad = jnp.concatenate([key_grad[:, h] for h in range(kv_heads)], 1)
    value_grad = jnp.concatenate([value_grad[:, h] for h in range(kv_heads)], 1)
    memory_key_grad, local_key = (key_grad[:count], key_grad[count:])
    memory_value_grad, local_value = (value_grad[:count], value_grad[count:])
    back_key, back_value = (
        lax.psum_scatter(memory_key_grad, "ctx", scatter_dimension=0, tiled=True),
        lax.psum_scatter(memory_value_grad, "ctx", scatter_dimension=0, tiled=True),
    )
    key_out = (
        local_key + lax.dynamic_update_slice_in_dim(jnp.zeros_like(local_key), back_key, length, 0)
    ).astype(jnp.bfloat16)
    value_result = (
        local_value
        + lax.dynamic_update_slice_in_dim(jnp.zeros_like(local_value), back_value, length, 0)
    ).astype(jnp.bfloat16)
    low_rank_rows = jnp.dot(
        hidden_row_block, adapter_down_weight, preferred_element_type=jnp.float32
    ).astype(jnp.bfloat16)
    packed = adapter_terms(hidden_row_block, low_rank_rows, value_result, adapter_up_weight)
    packed = mesh_sum(packed)
    model_width = hidden_row_block.shape[1]
    adapter_factor = adapter_scale / (log_batch * segment_list)
    down_sum = packed[:, :model_width].T
    up_sum = packed[:, model_width:]
    return (
        query_out[None, None],
        key_out[None, None],
        value_result[None, None],
        down_sum * adapter_factor,
        up_sum * adapter_factor,
    )


def solution(mesh):
    placed = (
        P("dp", "ctx", None, None),
        P("dp", "ctx", None, None),
        P("dp", "ctx", None, None),
        P("dp", "ctx", None, None),
        P("dp", "ctx", None, None),
        P(),
        P(),
        P("dp", "ctx"),
    )
    return jax.shard_map(
        per_device,
        mesh=mesh,
        in_specs=placed,
        out_specs=(
            P("dp", "ctx", None, None),
            P("dp", "ctx", None, None),
            P("dp", "ctx", None, None),
            P(),
            P(),
        ),
        check_vma=False,
    )
```

```python
import math

import jax
import numpy as np
import jax.numpy as jnp
from jax import lax
from jax.sharding import PartitionSpec as P

HEAD_SIZE = 128
SUMM = 50


adapter_scale = 2.0


def group_grads(query_group, key_group, value_group, cot_group, key_mask):
    softmax_scale = 1.0 / math.sqrt(HEAD_SIZE)
    scores = (
        jnp.einsum("tgd,md->gtm", query_group, key_group, preferred_element_type=jnp.float32)
        * softmax_scale
    )
    unnorm = jnp.exp(jnp.where(key_mask[None], scores, -jnp.inf))
    attend = unnorm / jnp.sum(unnorm, -1, keepdims=True)
    attend_grad = jnp.einsum(
        "tgd,md->gtm", cot_group, value_group, preferred_element_type=jnp.float32
    )
    row_dot = jnp.sum(attend * attend_grad, -1, keepdims=True)
    dscore = (attend * (attend_grad - row_dot)).astype(jnp.bfloat16)
    attend_low = attend.astype(jnp.bfloat16)
    query_grad = (
        jnp.einsum("gtm,md->tgd", dscore, key_group, preferred_element_type=jnp.float32)
        * softmax_scale
    )
    key_grad = (
        jnp.einsum("gtm,tgd->md", dscore, query_group, preferred_element_type=jnp.float32)
        * softmax_scale
    )
    value_grad = jnp.einsum(
        "gtm,tgd->md", attend_low, cot_group, preferred_element_type=jnp.float32
    )
    return (query_grad, key_grad, value_grad)


def adapter_terms(hidden_piece, low_rank_piece, value_piece, adapter_up_weight):
    contract = (((0,), (0,)), ((), ()))
    backward_step = lax.dot_general(
        value_piece, adapter_up_weight, (((1,), (1,)), ((), ())), preferred_element_type=jnp.float32
    ).astype(jnp.bfloat16)
    down_part_t = lax.dot_general(
        backward_step, hidden_piece, contract, preferred_element_type=jnp.float32
    )
    up_part = lax.dot_general(
        low_rank_piece, value_piece, contract, preferred_element_type=jnp.float32
    )
    return jnp.concatenate([down_part_t, up_part], 1)


def butterfly_sum(x, axis):
    n = lax.axis_size(axis)
    if n & (n - 1):
        return lax.psum(x, axis)
    k = 1
    while k < n:
        x = x + lax.ppermute(x, axis, [(i, i ^ k) for i in range(n)])
        k *= 2
    return x


def exchange_pairs(axis, k):
    return [(i, i ^ k) for i in range(lax.axis_size(axis))]


def mesh_sum(x):
    rounds = []
    for axis in ("dp", "ctx"):
        n = lax.axis_size(axis)
        if n & (n - 1):
            return lax.psum(x, ("dp", "ctx"))
        rounds += [(axis, 1 << j) for j in range(n.bit_length() - 1)]
    nearest = [r for r in (("dp", 1), ("dp", 2), ("ctx", 1), ("dp", 8)) if r in rounds]
    halving = [r for r in nearest if x.shape[-1] % (2 ** len(nearest)) == 0]
    cur = x
    for axis, k in halving:
        h = cur.shape[-1] // 2
        bit = (lax.axis_index(axis) // k) % 2
        keep = lax.dynamic_slice_in_dim(cur, bit * h, h, cur.ndim - 1)
        give = lax.dynamic_slice_in_dim(cur, (1 - bit) * h, h, cur.ndim - 1)
        cur = keep + lax.ppermute(give, axis, exchange_pairs(axis, k))
    for axis, k in rounds:
        if (axis, k) not in halving:
            cur = cur + lax.ppermute(cur, axis, exchange_pairs(axis, k))
    for axis, k in reversed(halving):
        bit = (lax.axis_index(axis) // k) % 2
        other = lax.ppermute(cur, axis, exchange_pairs(axis, k))
        cur = jnp.where(
            bit == 0, jnp.concatenate([cur, other], -1), jnp.concatenate([other, cur], -1)
        )
    return cur


def per_device(
    queries,
    rotated_key_rows,
    values,
    cotangent,
    hidden,
    adapter_down_weight,
    adapter_up_weight,
    segment_text_length,
):
    query_rows = queries[0, 0]
    key_local = rotated_key_rows[0, 0]
    value_local = values[0, 0]
    cot_rows = cotangent[0, 0]
    hidden_row_block = hidden[0, 0]
    length = segment_text_length[0, 0]
    position = lax.axis_index("ctx")
    segment_list = lax.axis_size("ctx")
    log_batch = lax.axis_size("dp")
    tokens = query_rows.shape[0]
    width = key_local.shape[1]
    kv_heads = width // HEAD_SIZE
    groups = query_rows.shape[1] // width
    live = length + SUMM
    rows = jnp.arange(tokens)
    cot_rows = jnp.where((rows < live)[:, None], cot_rows, jnp.zeros_like(cot_rows))
    own_keys = lax.dynamic_slice_in_dim(key_local, length, SUMM, 0)
    own_values = lax.dynamic_slice_in_dim(value_local, length, SUMM, 0)
    own_summary = jnp.concatenate([own_keys, own_values], 0)
    held = own_summary[None]
    distance_of_slot = [0]
    hop = segment_list // 2
    while hop >= 1:
        arrived = lax.ppermute(held, "ctx", [(i, i + hop) for i in range(segment_list - hop)])
        held = jnp.concatenate([held, arrived], 0)
        distance_of_slot = distance_of_slot + [d + hop for d in distance_of_slot]
        hop //= 2
    slot_of_distance = np.argsort(np.array(distance_of_slot)).astype(np.int32)
    slot_of_segment = jnp.asarray(slot_of_distance)[(position - jnp.arange(segment_list)) % segment_list]
    gathered = jnp.take(held, slot_of_segment, axis=0).reshape(segment_list, 2, SUMM, width)
    memory_keys = gathered[:, 0].reshape(segment_list * SUMM, width)
    memory_values = gathered[:, 1].reshape(segment_list * SUMM, width)
    count = memory_keys.shape[0]
    memory_owner = jnp.arange(count) // SUMM
    local_mask = (rows[None, :] <= rows[:, None]) & (rows[None, :] < live)
    memory_mask = jnp.broadcast_to((memory_owner < position)[None, :], (tokens, count))
    key_mask = jnp.concatenate([memory_mask, local_mask], axis=1)
    all_keys = jnp.concatenate([memory_keys, key_local], 0)
    all_values = jnp.concatenate([memory_values, value_local], 0)
    softmax_scale = 1.0 / math.sqrt(HEAD_SIZE)
    query_heads = query_rows.reshape(tokens, kv_heads, groups, HEAD_SIZE)
    cot_heads = cot_rows.reshape(tokens, kv_heads, groups, HEAD_SIZE)
    key_heads = all_keys.reshape(-1, kv_heads, HEAD_SIZE)
    value_heads = all_values.reshape(-1, kv_heads, HEAD_SIZE)
    scores = (
        jnp.einsum("tkgd,mkd->kgtm", query_heads, key_heads, preferred_element_type=jnp.float32)
        * softmax_scale
    )
    unnorm = jnp.exp(jnp.where(key_mask[None, None], scores, -jnp.inf))
    attend = unnorm / jnp.sum(unnorm, -1, keepdims=True)
    attend_grad = jnp.einsum(
        "tkgd,mkd->kgtm", cot_heads, value_heads, preferred_element_type=jnp.float32
    )
    row_dot = jnp.sum(attend * attend_grad, -1, keepdims=True)
    dscore = (attend * (attend_grad - row_dot)).astype(jnp.bfloat16)
    attend_low = attend.astype(jnp.bfloat16)
    query_out = (
        jnp.einsum("kgtm,mkd->tkgd", dscore, key_heads, preferred_element_type=jnp.float32)
        * softmax_scale
    ).reshape(tokens, kv_heads * groups * HEAD_SIZE).astype(jnp.bfloat16)
    key_grad = (
        jnp.einsum("kgtm,tkgd->mkd", dscore, query_heads, preferred_element_type=jnp.float32)
        * softmax_scale
    )
    value_grad = jnp.einsum(
        "kgtm,tkgd->mkd", attend_low, cot_heads, preferred_element_type=jnp.float32
    )
    key_grad = jnp.concatenate([key_grad[:, h] for h in range(kv_heads)], 1)
    value_grad = jnp.concatenate([value_grad[:, h] for h in range(kv_heads)], 1)
    memory_key_grad, local_key = (key_grad[:count], key_grad[count:])
    memory_value_grad, local_value = (value_grad[:count], value_grad[count:])
    back_key, back_value = (
        lax.psum_scatter(memory_key_grad, "ctx", scatter_dimension=0, tiled=True),
        lax.psum_scatter(memory_value_grad, "ctx", scatter_dimension=0, tiled=True),
    )
    key_out = (
        local_key + lax.dynamic_update_slice_in_dim(jnp.zeros_like(local_key), back_key, length, 0)
    ).astype(jnp.bfloat16)
    value_result = (
        local_value
        + lax.dynamic_update_slice_in_dim(jnp.zeros_like(local_value), back_value, length, 0)
    ).astype(jnp.bfloat16)
    low_rank_rows = jnp.dot(
        hidden_row_block, adapter_down_weight, preferred_element_type=jnp.float32
    ).astype(jnp.bfloat16)
    packed = adapter_terms(hidden_row_block, low_rank_rows, value_result, adapter_up_weight)
    packed = mesh_sum(packed)
    model_width = hidden_row_block.shape[1]
    adapter_factor = adapter_scale / (log_batch * segment_list)
    down_sum = packed[:, :model_width].T
    up_sum = packed[:, model_width:]
    return (
        query_out[None, None],
        key_out[None, None],
        value_result[None, None],
        down_sum * adapter_factor,
        up_sum * adapter_factor,
    )


def solution(mesh):
    placed = (
        P("dp", "ctx", None, None),
        P("dp", "ctx", None, None),
        P("dp", "ctx", None, None),
        P("dp", "ctx", None, None),
        P("dp", "ctx", None, None),
        P(),
        P(),
        P("dp", "ctx"),
    )
    return jax.shard_map(
        per_device,
        mesh=mesh,
        in_specs=placed,
        out_specs=(
            P("dp", "ctx", None, None),
            P("dp", "ctx", None, None),
            P("dp", "ctx", None, None),
            P(),
            P(),
        ),
        check_vma=False,
    )
```

```python
import math

import jax
import numpy as np
import jax.numpy as jnp
from jax import lax
from jax.sharding import PartitionSpec as P

HEAD_SIZE = 128
SUMM = 50


adapter_scale = 2.0


def group_grads(query_group, key_group, value_group, cot_group, key_mask):
    softmax_scale = 1.0 / math.sqrt(HEAD_SIZE)
    scores = (
        jnp.einsum("tgd,md->gtm", query_group, key_group, preferred_element_type=jnp.float32)
        * softmax_scale
    )
    unnorm = jnp.exp(jnp.where(key_mask[None], scores, -jnp.inf))
    attend = unnorm / jnp.sum(unnorm, -1, keepdims=True)
    attend_grad = jnp.einsum(
        "tgd,md->gtm", cot_group, value_group, preferred_element_type=jnp.float32
    )
    row_dot = jnp.sum(attend * attend_grad, -1, keepdims=True)
    dscore = (attend * (attend_grad - row_dot)).astype(jnp.bfloat16)
    attend_low = attend.astype(jnp.bfloat16)
    query_grad = (
        jnp.einsum("gtm,md->tgd", dscore, key_group, preferred_element_type=jnp.float32)
        * softmax_scale
    )
    key_grad = (
        jnp.einsum("gtm,tgd->md", dscore, query_group, preferred_element_type=jnp.float32)
        * softmax_scale
    )
    value_grad = jnp.einsum(
        "gtm,tgd->md", attend_low, cot_group, preferred_element_type=jnp.float32
    )
    return (query_grad, key_grad, value_grad)


def adapter_terms(hidden_piece, low_rank_piece, value_piece, adapter_up_weight):
    contract = (((0,), (0,)), ((), ()))
    backward_step = lax.dot_general(
        value_piece, adapter_up_weight, (((1,), (1,)), ((), ())), preferred_element_type=jnp.float32
    ).astype(jnp.bfloat16)
    down_part_t = lax.dot_general(
        backward_step, hidden_piece, contract, preferred_element_type=jnp.float32
    )
    up_part = lax.dot_general(
        low_rank_piece, value_piece, contract, preferred_element_type=jnp.float32
    )
    return jnp.concatenate([down_part_t, up_part], 1)


def butterfly_sum(x, axis):
    n = lax.axis_size(axis)
    if n & (n - 1):
        return lax.psum(x, axis)
    k = 1
    while k < n:
        x = x + lax.ppermute(x, axis, [(i, i ^ k) for i in range(n)])
        k *= 2
    return x


def exchange_pairs(axis, k):
    return [(i, i ^ k) for i in range(lax.axis_size(axis))]


def mesh_sum(x):
    rounds = []
    for axis in ("dp", "ctx"):
        n = lax.axis_size(axis)
        if n & (n - 1):
            return lax.psum(x, ("dp", "ctx"))
        rounds += [(axis, 1 << j) for j in range(n.bit_length() - 1)]
    nearest = [r for r in (("dp", 1), ("dp", 2), ("ctx", 1)) if r in rounds]
    halving = [r for r in nearest if x.shape[-1] % (2 ** len(nearest)) == 0]
    cur = x
    for axis, k in halving:
        h = cur.shape[-1] // 2
        bit = (lax.axis_index(axis) // k) % 2
        keep = lax.dynamic_slice_in_dim(cur, bit * h, h, cur.ndim - 1)
        give = lax.dynamic_slice_in_dim(cur, (1 - bit) * h, h, cur.ndim - 1)
        cur = keep + lax.ppermute(give, axis, exchange_pairs(axis, k))
    for axis, k in rounds:
        if (axis, k) not in halving:
            cur = cur + lax.ppermute(cur, axis, exchange_pairs(axis, k))
    for axis, k in reversed(halving):
        bit = (lax.axis_index(axis) // k) % 2
        other = lax.ppermute(cur, axis, exchange_pairs(axis, k))
        h = cur.shape[-1]
        joined = jnp.zeros(cur.shape[:-1] + (2 * h,), cur.dtype)
        joined = lax.dynamic_update_slice_in_dim(joined, cur, bit * h, cur.ndim - 1)
        cur = lax.dynamic_update_slice_in_dim(joined, other, (1 - bit) * h, cur.ndim - 1)
    return cur


def per_device(
    queries,
    rotated_key_rows,
    values,
    cotangent,
    hidden,
    adapter_down_weight,
    adapter_up_weight,
    segment_text_length,
):
    query_rows = queries[0, 0]
    key_local = rotated_key_rows[0, 0]
    value_local = values[0, 0]
    cot_rows = cotangent[0, 0]
    hidden_row_block = hidden[0, 0]
    length = segment_text_length[0, 0]
    position = lax.axis_index("ctx")
    segment_list = lax.axis_size("ctx")
    log_batch = lax.axis_size("dp")
    tokens = query_rows.shape[0]
    width = key_local.shape[1]
    kv_heads = width // HEAD_SIZE
    groups = query_rows.shape[1] // width
    live = length + SUMM
    rows = jnp.arange(tokens)
    cot_rows = jnp.where((rows < live)[:, None], cot_rows, jnp.zeros_like(cot_rows))
    own_keys = lax.dynamic_slice_in_dim(key_local, length, SUMM, 0)
    own_values = lax.dynamic_slice_in_dim(value_local, length, SUMM, 0)
    own_summary = jnp.concatenate([own_keys, own_values], 0)
    held = own_summary[None]
    distance_of_slot = [0]
    hop = segment_list // 2
    while hop >= 1:
        arrived = lax.ppermute(held, "ctx", [(i, i + hop) for i in range(segment_list - hop)])
        held = jnp.concatenate([held, arrived], 0)
        distance_of_slot = distance_of_slot + [d + hop for d in distance_of_slot]
        hop //= 2
    slot_of_distance = np.argsort(np.array(distance_of_slot)).astype(np.int32)
    slot_of_segment = jnp.asarray(slot_of_distance)[(position - jnp.arange(segment_list)) % segment_list]
    gathered = jnp.take(held, slot_of_segment, axis=0).reshape(segment_list, 2, SUMM, width)
    memory_keys = gathered[:, 0].reshape(segment_list * SUMM, width)
    memory_values = gathered[:, 1].reshape(segment_list * SUMM, width)
    count = memory_keys.shape[0]
    memory_owner = jnp.arange(count) // SUMM
    local_mask = (rows[None, :] <= rows[:, None]) & (rows[None, :] < live)
    memory_mask = jnp.broadcast_to((memory_owner < position)[None, :], (tokens, count))
    key_mask = jnp.concatenate([memory_mask, local_mask], axis=1)
    all_keys = jnp.concatenate([memory_keys, key_local], 0)
    all_values = jnp.concatenate([memory_values, value_local], 0)
    softmax_scale = 1.0 / math.sqrt(HEAD_SIZE)
    query_heads = query_rows.reshape(tokens, kv_heads, groups, HEAD_SIZE)
    cot_heads = cot_rows.reshape(tokens, kv_heads, groups, HEAD_SIZE)
    key_heads = all_keys.reshape(-1, kv_heads, HEAD_SIZE)
    value_heads = all_values.reshape(-1, kv_heads, HEAD_SIZE)
    scores = (
        jnp.einsum("tkgd,mkd->kgtm", query_heads, key_heads, preferred_element_type=jnp.float32)
        * softmax_scale
    )
    unnorm = jnp.exp(jnp.where(key_mask[None, None], scores, -jnp.inf))
    attend = unnorm / jnp.sum(unnorm, -1, keepdims=True)
    attend_grad = jnp.einsum(
        "tkgd,mkd->kgtm", cot_heads, value_heads, preferred_element_type=jnp.float32
    )
    row_dot = jnp.sum(attend * attend_grad, -1, keepdims=True)
    dscore = (attend * (attend_grad - row_dot)).astype(jnp.bfloat16)
    attend_low = attend.astype(jnp.bfloat16)
    query_out = (
        jnp.einsum("kgtm,mkd->tkgd", dscore, key_heads, preferred_element_type=jnp.float32)
        * softmax_scale
    ).reshape(tokens, kv_heads * groups * HEAD_SIZE).astype(jnp.bfloat16)
    key_grad = (
        jnp.einsum("kgtm,tkgd->mkd", dscore, query_heads, preferred_element_type=jnp.float32)
        * softmax_scale
    )
    value_grad = jnp.einsum(
        "kgtm,tkgd->mkd", attend_low, cot_heads, preferred_element_type=jnp.float32
    )
    key_grad = jnp.concatenate([key_grad[:, h] for h in range(kv_heads)], 1)
    value_grad = jnp.concatenate([value_grad[:, h] for h in range(kv_heads)], 1)
    memory_key_grad, local_key = (key_grad[:count], key_grad[count:])
    memory_value_grad, local_value = (value_grad[:count], value_grad[count:])
    back_key, back_value = (
        lax.psum_scatter(memory_key_grad, "ctx", scatter_dimension=0, tiled=True),
        lax.psum_scatter(memory_value_grad, "ctx", scatter_dimension=0, tiled=True),
    )
    key_out = (
        local_key + lax.dynamic_update_slice_in_dim(jnp.zeros_like(local_key), back_key, length, 0)
    ).astype(jnp.bfloat16)
    value_result = (
        local_value
        + lax.dynamic_update_slice_in_dim(jnp.zeros_like(local_value), back_value, length, 0)
    ).astype(jnp.bfloat16)
    low_rank_rows = jnp.dot(
        hidden_row_block, adapter_down_weight, preferred_element_type=jnp.float32
    ).astype(jnp.bfloat16)
    packed = adapter_terms(hidden_row_block, low_rank_rows, value_result, adapter_up_weight)
    packed = mesh_sum(packed)
    model_width = hidden_row_block.shape[1]
    adapter_factor = adapter_scale / (log_batch * segment_list)
    down_sum = packed[:, :model_width].T
    up_sum = packed[:, model_width:]
    return (
        query_out[None, None],
        key_out[None, None],
        value_result[None, None],
        down_sum * adapter_factor,
        up_sum * adapter_factor,
    )


def solution(mesh):
    placed = (
        P("dp", "ctx", None, None),
        P("dp", "ctx", None, None),
        P("dp", "ctx", None, None),
        P("dp", "ctx", None, None),
        P("dp", "ctx", None, None),
        P(),
        P(),
        P("dp", "ctx"),
    )
    return jax.shard_map(
        per_device,
        mesh=mesh,
        in_specs=placed,
        out_specs=(
            P("dp", "ctx", None, None),
            P("dp", "ctx", None, None),
            P("dp", "ctx", None, None),
            P(),
            P(),
        ),
        check_vma=False,
    )
```

```python
import math

import jax
import numpy as np
import jax.numpy as jnp
from jax import lax
from jax.sharding import PartitionSpec as P

HEAD_SIZE = 128
SUMM = 50


adapter_scale = 2.0


def group_grads(query_group, key_group, value_group, cot_group, key_mask):
    softmax_scale = 1.0 / math.sqrt(HEAD_SIZE)
    scores = (
        jnp.einsum("tgd,md->gtm", query_group, key_group, preferred_element_type=jnp.float32)
        * softmax_scale
    )
    unnorm = jnp.exp(jnp.where(key_mask[None], scores, -jnp.inf))
    attend = unnorm / jnp.sum(unnorm, -1, keepdims=True)
    attend_grad = jnp.einsum(
        "tgd,md->gtm", cot_group, value_group, preferred_element_type=jnp.float32
    )
    row_dot = jnp.sum(attend * attend_grad, -1, keepdims=True)
    dscore = (attend * (attend_grad - row_dot)).astype(jnp.bfloat16)
    attend_low = attend.astype(jnp.bfloat16)
    query_grad = (
        jnp.einsum("gtm,md->tgd", dscore, key_group, preferred_element_type=jnp.float32)
        * softmax_scale
    )
    key_grad = (
        jnp.einsum("gtm,tgd->md", dscore, query_group, preferred_element_type=jnp.float32)
        * softmax_scale
    )
    value_grad = jnp.einsum(
        "gtm,tgd->md", attend_low, cot_group, preferred_element_type=jnp.float32
    )
    return (query_grad, key_grad, value_grad)


def adapter_terms(hidden_piece, low_rank_piece, value_piece, adapter_up_weight):
    contract = (((0,), (0,)), ((), ()))
    backward_step = lax.dot_general(
        value_piece, adapter_up_weight, (((1,), (1,)), ((), ())), preferred_element_type=jnp.float32
    ).astype(jnp.bfloat16)
    down_part_t = lax.dot_general(
        backward_step, hidden_piece, contract, preferred_element_type=jnp.float32
    )
    up_part = lax.dot_general(
        low_rank_piece, value_piece, contract, preferred_element_type=jnp.float32
    )
    return jnp.concatenate([down_part_t, up_part], 1)


def butterfly_sum(x, axis):
    n = lax.axis_size(axis)
    if n & (n - 1):
        return lax.psum(x, axis)
    k = 1
    while k < n:
        x = x + lax.ppermute(x, axis, [(i, i ^ k) for i in range(n)])
        k *= 2
    return x


def exchange_pairs(axis, k):
    return [(i, i ^ k) for i in range(lax.axis_size(axis))]


def mesh_sum(x):
    rounds = []
    for axis in ("dp", "ctx"):
        n = lax.axis_size(axis)
        if n & (n - 1):
            return lax.psum(x, ("dp", "ctx"))
        rounds += [(axis, 1 << j) for j in range(n.bit_length() - 1)]
    nearest = [r for r in (("dp", 1), ("ctx", 1), ("dp", 2)) if r in rounds]
    halving = [r for r in nearest if x.shape[-1] % (2 ** len(nearest)) == 0]
    cur = x
    for axis, k in halving:
        h = cur.shape[-1] // 2
        bit = (lax.axis_index(axis) // k) % 2
        keep = lax.dynamic_slice_in_dim(cur, bit * h, h, cur.ndim - 1)
        give = lax.dynamic_slice_in_dim(cur, (1 - bit) * h, h, cur.ndim - 1)
        cur = keep + lax.ppermute(give, axis, exchange_pairs(axis, k))
    for axis, k in rounds:
        if (axis, k) not in halving:
            cur = cur + lax.ppermute(cur, axis, exchange_pairs(axis, k))
    for axis, k in reversed(halving):
        bit = (lax.axis_index(axis) // k) % 2
        other = lax.ppermute(cur, axis, exchange_pairs(axis, k))
        cur = jnp.where(
            bit == 0, jnp.concatenate([cur, other], -1), jnp.concatenate([other, cur], -1)
        )
    return cur


def per_device(
    queries,
    rotated_key_rows,
    values,
    cotangent,
    hidden,
    adapter_down_weight,
    adapter_up_weight,
    segment_text_length,
):
    query_rows = queries[0, 0]
    key_local = rotated_key_rows[0, 0]
    value_local = values[0, 0]
    cot_rows = cotangent[0, 0]
    hidden_row_block = hidden[0, 0]
    length = segment_text_length[0, 0]
    position = lax.axis_index("ctx")
    segment_list = lax.axis_size("ctx")
    log_batch = lax.axis_size("dp")
    tokens = query_rows.shape[0]
    width = key_local.shape[1]
    kv_heads = width // HEAD_SIZE
    groups = query_rows.shape[1] // width
    live = length + SUMM
    rows = jnp.arange(tokens)
    cot_rows = jnp.where((rows < live)[:, None], cot_rows, jnp.zeros_like(cot_rows))
    own_keys = lax.dynamic_slice_in_dim(key_local, length, SUMM, 0)
    own_values = lax.dynamic_slice_in_dim(value_local, length, SUMM, 0)
    own_summary = jnp.concatenate([own_keys, own_values], 0)
    held = own_summary[None]
    distance_of_slot = [0]
    hop = segment_list // 2
    while hop >= 1:
        arrived = lax.ppermute(held, "ctx", [(i, i + hop) for i in range(segment_list - hop)])
        held = jnp.concatenate([held, arrived], 0)
        distance_of_slot = distance_of_slot + [d + hop for d in distance_of_slot]
        hop //= 2
    slot_of_distance = np.argsort(np.array(distance_of_slot)).astype(np.int32)
    slot_of_segment = jnp.asarray(slot_of_distance)[(position - jnp.arange(segment_list)) % segment_list]
    gathered = jnp.take(held, slot_of_segment, axis=0).reshape(segment_list, 2, SUMM, width)
    memory_keys = gathered[:, 0].reshape(segment_list * SUMM, width)
    memory_values = gathered[:, 1].reshape(segment_list * SUMM, width)
    count = memory_keys.shape[0]
    memory_owner = jnp.arange(count) // SUMM
    local_mask = (rows[None, :] <= rows[:, None]) & (rows[None, :] < live)
    memory_mask = jnp.broadcast_to((memory_owner < position)[None, :], (tokens, count))
    key_mask = jnp.concatenate([memory_mask, local_mask], axis=1)
    all_keys = jnp.concatenate([memory_keys, key_local], 0)
    all_values = jnp.concatenate([memory_values, value_local], 0)
    softmax_scale = 1.0 / math.sqrt(HEAD_SIZE)
    query_heads = query_rows.reshape(tokens, kv_heads, groups, HEAD_SIZE)
    cot_heads = cot_rows.reshape(tokens, kv_heads, groups, HEAD_SIZE)
    key_heads = all_keys.reshape(-1, kv_heads, HEAD_SIZE)
    value_heads = all_values.reshape(-1, kv_heads, HEAD_SIZE)
    scores = (
        jnp.einsum("tkgd,mkd->kgtm", query_heads, key_heads, preferred_element_type=jnp.float32)
        * softmax_scale
    )
    unnorm = jnp.exp(jnp.where(key_mask[None, None], scores, -jnp.inf))
    attend = unnorm / jnp.sum(unnorm, -1, keepdims=True)
    attend_grad = jnp.einsum(
        "tkgd,mkd->kgtm", cot_heads, value_heads, preferred_element_type=jnp.float32
    )
    row_dot = jnp.sum(attend * attend_grad, -1, keepdims=True)
    dscore = (attend * (attend_grad - row_dot)).astype(jnp.bfloat16)
    attend_low = attend.astype(jnp.bfloat16)
    query_out = (
        jnp.einsum("kgtm,mkd->tkgd", dscore, key_heads, preferred_element_type=jnp.float32)
        * softmax_scale
    ).reshape(tokens, kv_heads * groups * HEAD_SIZE).astype(jnp.bfloat16)
    key_grad = (
        jnp.einsum("kgtm,tkgd->mkd", dscore, query_heads, preferred_element_type=jnp.float32)
        * softmax_scale
    )
    value_grad = jnp.einsum(
        "kgtm,tkgd->mkd", attend_low, cot_heads, preferred_element_type=jnp.float32
    )
    key_grad = jnp.concatenate([key_grad[:, h] for h in range(kv_heads)], 1)
    value_grad = jnp.concatenate([value_grad[:, h] for h in range(kv_heads)], 1)
    memory_key_grad, local_key = (key_grad[:count], key_grad[count:])
    memory_value_grad, local_value = (value_grad[:count], value_grad[count:])
    back_key, back_value = (
        lax.psum_scatter(memory_key_grad, "ctx", scatter_dimension=0, tiled=True),
        lax.psum_scatter(memory_value_grad, "ctx", scatter_dimension=0, tiled=True),
    )
    key_out = (
        local_key + lax.dynamic_update_slice_in_dim(jnp.zeros_like(local_key), back_key, length, 0)
    ).astype(jnp.bfloat16)
    value_result = (
        local_value
        + lax.dynamic_update_slice_in_dim(jnp.zeros_like(local_value), back_value, length, 0)
    ).astype(jnp.bfloat16)
    low_rank_rows = jnp.dot(
        hidden_row_block, adapter_down_weight, preferred_element_type=jnp.float32
    ).astype(jnp.bfloat16)
    packed = adapter_terms(hidden_row_block, low_rank_rows, value_result, adapter_up_weight)
    packed = mesh_sum(packed)
    model_width = hidden_row_block.shape[1]
    adapter_factor = adapter_scale / (log_batch * segment_list)
    down_sum = packed[:, :model_width].T
    up_sum = packed[:, model_width:]
    return (
        query_out[None, None],
        key_out[None, None],
        value_result[None, None],
        down_sum * adapter_factor,
        up_sum * adapter_factor,
    )


def solution(mesh):
    placed = (
        P("dp", "ctx", None, None),
        P("dp", "ctx", None, None),
        P("dp", "ctx", None, None),
        P("dp", "ctx", None, None),
        P("dp", "ctx", None, None),
        P(),
        P(),
        P("dp", "ctx"),
    )
    return jax.shard_map(
        per_device,
        mesh=mesh,
        in_specs=placed,
        out_specs=(
            P("dp", "ctx", None, None),
            P("dp", "ctx", None, None),
            P("dp", "ctx", None, None),
            P(),
            P(),
        ),
        check_vma=False,
    )
```

```python
import math

import jax
import numpy as np
import jax.numpy as jnp
from jax import lax
from jax.sharding import PartitionSpec as P

HEAD_SIZE = 128
SUMM = 50


adapter_scale = 2.0


def group_grads(query_group, key_group, value_group, cot_group, key_mask):
    softmax_scale = 1.0 / math.sqrt(HEAD_SIZE)
    scores = (
        jnp.einsum("tgd,md->gtm", query_group, key_group, preferred_element_type=jnp.float32)
        * softmax_scale
    )
    unnorm = jnp.exp(jnp.where(key_mask[None], scores, -jnp.inf))
    attend = unnorm / jnp.sum(unnorm, -1, keepdims=True)
    attend_grad = jnp.einsum(
        "tgd,md->gtm", cot_group, value_group, preferred_element_type=jnp.float32
    )
    row_dot = jnp.sum(attend * attend_grad, -1, keepdims=True)
    dscore = (attend * (attend_grad - row_dot)).astype(jnp.bfloat16)
    attend_low = attend.astype(jnp.bfloat16)
    query_grad = (
        jnp.einsum("gtm,md->tgd", dscore, key_group, preferred_element_type=jnp.float32)
        * softmax_scale
    )
    key_grad = (
        jnp.einsum("gtm,tgd->md", dscore, query_group, preferred_element_type=jnp.float32)
        * softmax_scale
    )
    value_grad = jnp.einsum(
        "gtm,tgd->md", attend_low, cot_group, preferred_element_type=jnp.float32
    )
    return (query_grad, key_grad, value_grad)


def adapter_terms(hidden_piece, low_rank_piece, value_piece, adapter_up_weight):
    contract = (((0,), (0,)), ((), ()))
    backward_step = lax.dot_general(
        value_piece, adapter_up_weight, (((1,), (1,)), ((), ())), preferred_element_type=jnp.float32
    ).astype(jnp.bfloat16)
    down_part_t = lax.dot_general(
        backward_step, hidden_piece, contract, preferred_element_type=jnp.float32
    )
    up_part = lax.dot_general(
        low_rank_piece, value_piece, contract, preferred_element_type=jnp.float32
    )
    return jnp.concatenate([down_part_t, up_part], 1)


def butterfly_sum(x, axis):
    n = lax.axis_size(axis)
    if n & (n - 1):
        return lax.psum(x, axis)
    k = 1
    while k < n:
        x = x + lax.ppermute(x, axis, [(i, i ^ k) for i in range(n)])
        k *= 2
    return x


def exchange_pairs(axis, k):
    return [(i, i ^ k) for i in range(lax.axis_size(axis))]


def mesh_sum(x):
    rounds = []
    for axis in ("dp", "ctx"):
        n = lax.axis_size(axis)
        if n & (n - 1):
            return lax.psum(x, ("dp", "ctx"))
        rounds += [(axis, 1 << j) for j in range(n.bit_length() - 1)]
    nearest = [r for r in (("dp", 1), ("ctx", 1), ("dp", 2), ("dp", 8)) if r in rounds]
    halving = [r for r in nearest if x.shape[-1] % (2 ** len(nearest)) == 0]
    cur = x
    for axis, k in halving:
        h = cur.shape[-1] // 2
        bit = (lax.axis_index(axis) // k) % 2
        keep = lax.dynamic_slice_in_dim(cur, bit * h, h, cur.ndim - 1)
        give = lax.dynamic_slice_in_dim(cur, (1 - bit) * h, h, cur.ndim - 1)
        cur = keep + lax.ppermute(give, axis, exchange_pairs(axis, k))
    for axis, k in rounds:
        if (axis, k) not in halving:
            cur = cur + lax.ppermute(cur, axis, exchange_pairs(axis, k))
    for axis, k in reversed(halving):
        bit = (lax.axis_index(axis) // k) % 2
        other = lax.ppermute(cur, axis, exchange_pairs(axis, k))
        cur = jnp.where(
            bit == 0, jnp.concatenate([cur, other], -1), jnp.concatenate([other, cur], -1)
        )
    return cur


def per_device(
    queries,
    rotated_key_rows,
    values,
    cotangent,
    hidden,
    adapter_down_weight,
    adapter_up_weight,
    segment_text_length,
):
    query_rows = queries[0, 0]
    key_local = rotated_key_rows[0, 0]
    value_local = values[0, 0]
    cot_rows = cotangent[0, 0]
    hidden_row_block = hidden[0, 0]
    length = segment_text_length[0, 0]
    position = lax.axis_index("ctx")
    segment_list = lax.axis_size("ctx")
    log_batch = lax.axis_size("dp")
    tokens = query_rows.shape[0]
    width = key_local.shape[1]
    kv_heads = width // HEAD_SIZE
    groups = query_rows.shape[1] // width
    live = length + SUMM
    rows = jnp.arange(tokens)
    cot_rows = jnp.where((rows < live)[:, None], cot_rows, jnp.zeros_like(cot_rows))
    own_keys = lax.dynamic_slice_in_dim(key_local, length, SUMM, 0)
    own_values = lax.dynamic_slice_in_dim(value_local, length, SUMM, 0)
    own_summary = jnp.concatenate([own_keys, own_values], 0)
    held = own_summary[None]
    distance_of_slot = [0]
    hop = segment_list // 2
    while hop >= 1:
        arrived = lax.ppermute(held, "ctx", [(i, i + hop) for i in range(segment_list - hop)])
        held = jnp.concatenate([held, arrived], 0)
        distance_of_slot = distance_of_slot + [d + hop for d in distance_of_slot]
        hop //= 2
    slot_of_distance = np.argsort(np.array(distance_of_slot)).astype(np.int32)
    slot_of_segment = jnp.asarray(slot_of_distance)[(position - jnp.arange(segment_list)) % segment_list]
    gathered = jnp.take(held, slot_of_segment, axis=0).reshape(segment_list, 2, SUMM, width)
    memory_keys = gathered[:, 0].reshape(segment_list * SUMM, width)
    memory_values = gathered[:, 1].reshape(segment_list * SUMM, width)
    count = memory_keys.shape[0]
    memory_owner = jnp.arange(count) // SUMM
    local_mask = (rows[None, :] <= rows[:, None]) & (rows[None, :] < live)
    memory_mask = jnp.broadcast_to((memory_owner < position)[None, :], (tokens, count))
    key_mask = jnp.concatenate([memory_mask, local_mask], axis=1)
    all_keys = jnp.concatenate([memory_keys, key_local], 0)
    all_values = jnp.concatenate([memory_values, value_local], 0)
    softmax_scale = 1.0 / math.sqrt(HEAD_SIZE)
    query_heads = query_rows.reshape(tokens, kv_heads, groups, HEAD_SIZE)
    cot_heads = cot_rows.reshape(tokens, kv_heads, groups, HEAD_SIZE)
    key_heads = all_keys.reshape(-1, kv_heads, HEAD_SIZE)
    value_heads = all_values.reshape(-1, kv_heads, HEAD_SIZE)
    scores = (
        jnp.einsum("tkgd,mkd->kgtm", query_heads, key_heads, preferred_element_type=jnp.float32)
        * softmax_scale
    )
    unnorm = jnp.exp(jnp.where(key_mask[None, None], scores, -jnp.inf))
    attend = unnorm / jnp.sum(unnorm, -1, keepdims=True)
    attend_grad = jnp.einsum(
        "tkgd,mkd->kgtm", cot_heads, value_heads, preferred_element_type=jnp.float32
    )
    row_dot = jnp.sum(attend * attend_grad, -1, keepdims=True)
    dscore = (attend * (attend_grad - row_dot)).astype(jnp.bfloat16)
    attend_low = attend.astype(jnp.bfloat16)
    query_out = (
        jnp.einsum("kgtm,mkd->tkgd", dscore, key_heads, preferred_element_type=jnp.float32)
        * softmax_scale
    ).reshape(tokens, kv_heads * groups * HEAD_SIZE).astype(jnp.bfloat16)
    key_grad = (
        jnp.einsum("kgtm,tkgd->mkd", dscore, query_heads, preferred_element_type=jnp.float32)
        * softmax_scale
    )
    value_grad = jnp.einsum(
        "kgtm,tkgd->mkd", attend_low, cot_heads, preferred_element_type=jnp.float32
    )
    key_grad = jnp.concatenate([key_grad[:, h] for h in range(kv_heads)], 1)
    value_grad = jnp.concatenate([value_grad[:, h] for h in range(kv_heads)], 1)
    memory_key_grad, local_key = (key_grad[:count], key_grad[count:])
    memory_value_grad, local_value = (value_grad[:count], value_grad[count:])
    back_key, back_value = (
        lax.psum_scatter(memory_key_grad, "ctx", scatter_dimension=0, tiled=True),
        lax.psum_scatter(memory_value_grad, "ctx", scatter_dimension=0, tiled=True),
    )
    key_out = (
        local_key + lax.dynamic_update_slice_in_dim(jnp.zeros_like(local_key), back_key, length, 0)
    ).astype(jnp.bfloat16)
    value_result = (
        local_value
        + lax.dynamic_update_slice_in_dim(jnp.zeros_like(local_value), back_value, length, 0)
    ).astype(jnp.bfloat16)
    low_rank_rows = jnp.dot(
        hidden_row_block, adapter_down_weight, preferred_element_type=jnp.float32
    ).astype(jnp.bfloat16)
    packed = adapter_terms(hidden_row_block, low_rank_rows, value_result, adapter_up_weight)
    packed = mesh_sum(packed)
    model_width = hidden_row_block.shape[1]
    adapter_factor = adapter_scale / (log_batch * segment_list)
    down_sum = packed[:, :model_width].T
    up_sum = packed[:, model_width:]
    return (
        query_out[None, None],
        key_out[None, None],
        value_result[None, None],
        down_sum * adapter_factor,
        up_sum * adapter_factor,
    )


def solution(mesh):
    placed = (
        P("dp", "ctx", None, None),
        P("dp", "ctx", None, None),
        P("dp", "ctx", None, None),
        P("dp", "ctx", None, None),
        P("dp", "ctx", None, None),
        P(),
        P(),
        P("dp", "ctx"),
    )
    return jax.shard_map(
        per_device,
        mesh=mesh,
        in_specs=placed,
        out_specs=(
            P("dp", "ctx", None, None),
            P("dp", "ctx", None, None),
            P("dp", "ctx", None, None),
            P(),
            P(),
        ),
        check_vma=False,
    )
```
